128 devices in a mesh: row: 32 (over y, x, core), head: 4 (over z).
Axes of the slice: x: 4, y: 4, z: 4, core: 2. Of those that a mesh axis runs over, the one named last changes fastest.
Arguments:
- features: bfloat16 [16384, 1024], P('row'), may hold values from -6 to 6
- w_qkv: bfloat16 [3, 1024, 1024], P(None, None, 'head'), may hold values from -0.1875 to 0.1875
- w_out: bfloat16 [1024, 1024], P('head'), may hold values from -0.1875 to 0.1875
- bias_gain: float32 [16], P('head'), may hold values from 0.5 to 1.5
- edge_bias: bfloat16 [256, 64, 4096], P('row'), may hold values from -6 to 250
- neighbours: int32 [256, 64], P('row'), may hold values from 0 to 255, as said below
- counts: int32 [256], P('row'), may hold values from 1 to 64, as said below
Outputs:
- mixed: bfloat16 [16384, 1024], P('row', 'head')
The draws below stay inside these ranges and needn't reach their ends.
Inputs may be any that keep to these rules, and one draw needn't show every extreme that they name: `neighbours`: key block b is owned by row device b // 8. Over all slots of the query blocks of one row device, at most 2 distinct key blocks of any one owner are named, and for every row device some owner has exactly 2. `counts`: the first query block of every row device has all 64 slots live.
All inputs are finite; a program needn't handle non-finite values.
Results may differ from the reference program's by a relative error of at most 0.011.
Values may be sent and summed in bfloat16 or wider, within the bound.
No kernel may reach another device: no remote copies, remote signals or barrier semaphores. Data moves between devices by JAX's collectives and lax.ppermute only.
A program may use at most 256 MiB of HBM per device.

```python
import math
import jax
import jax.numpy as jnp
from jax import lax

D = 1024
HEADS = 16
HD = 64
BLK = 64
NB = 64
QB_DEV = 8
CAP = 2
NODES = 16384
QBLOCKS = 256


def plan_lists(key):
    owners = QBLOCKS // QB_DEV
    base = jax.random.fold_in(key, 7001)
    perm_keys = jax.random.split(jax.random.fold_in(base, 1), owners * owners)
    perms = jax.vmap(lambda subkey: jax.random.permutation(subkey, QB_DEV))(perm_keys)
    perms = perms.reshape(owners, owners, QB_DEV)[:, :, :CAP]
    candidate = perms + (jnp.arange(owners, dtype=jnp.int32) * QB_DEV)[None, :, None]
    candidate = candidate.reshape(owners, owners * CAP)
    picks = jax.random.randint(jax.random.fold_in(base, 2), (owners, QB_DEV, NB), 0, owners * CAP)
    forced_owner = jax.random.randint(jax.random.fold_in(base, 3), (owners,), 0, owners)
    forced = forced_owner[:, None] * CAP + jnp.arange(CAP, dtype=jnp.int32)[None, :]
    picks = picks.at[:, 0, :CAP].set(forced)
    block_ids = jnp.take_along_axis(candidate, picks.reshape(owners, QB_DEV * NB), axis=1)
    block_ids = block_ids.reshape(QBLOCKS, NB)
    levels = jax.random.randint(jax.random.fold_in(base, 4), (owners, 1), 1, NB + 1)
    raw_counts = jax.random.randint(jax.random.fold_in(base, 5), (owners, QB_DEV), 0, NB + 1)
    live_counts = jnp.maximum(levels, raw_counts)
    live_counts = live_counts.at[:, 0].set(NB)
    return (block_ids.astype(jnp.int32), live_counts.reshape(QBLOCKS).astype(jnp.int32))


def draw_neighbours(key, part):
    return plan_lists(key)[0]


def draw_counts(key, part):
    return plan_lists(key)[1]


def draw_edge_bias(key, part):
    shape = (QBLOCKS, BLK, NB * BLK)
    return jnp.clip(jax.random.normal(key, shape, jnp.float32), -6.0, 6.0).astype(jnp.bfloat16)


def block_scale(own_key, extent, shards, least, top_value):
    loudness, own = 1.0, jax.random.fold_in(own_key, 6)
    for axis_at, parts in shards:
        draws = jnp.exp(jax.random.uniform(jax.random.fold_in(own, axis_at), (parts,), jnp.float32, least / len(shards), top_value / len(shards)))
        loudness = loudness * jnp.repeat(draws, extent[axis_at] // parts).reshape([-1 if axis == axis_at else 1 for axis in range(len(extent))])
    return loudness


def scatter_about(own_key, dims, scale, bound, shards=(), kind=jnp.bfloat16):
    drawn = jax.random.normal(own_key, dims, jnp.float32) * scale
    if len(shards) > 0:
        drawn = block_scale(own_key, dims, shards, -0.22, 0.18) * drawn
    return jnp.clip(drawn, min=-bound, max=bound).astype(kind)


def setup_inputs(seed: int = 0) -> dict:
    key_list = jax.random.split(jax.random.key(seed), 8)
    features = scatter_about(key_list[0], (NODES, D), 1.0, 6.0, ((0, 32),))
    w_qkv = scatter_about(key_list[1], (3, D, HEADS * HD), D ** -0.5, 0.1875, ((2, 4),))
    w_out = scatter_about(key_list[2], (HEADS * HD, D), (HEADS * HD) ** -0.5, 0.1875, ((0, 4),))
    bias_gain = jnp.clip(jnp.exp(math.log(1.5) - 1.0986123 * jax.random.uniform(key_list[3], (HEADS,), jnp.float32) ** block_scale(key_list[3], (HEADS,), ((0, 4),), -0.2, 0.2)), 0.5, 1.5)
    edge_bias = draw_edge_bias(jax.random.fold_in(key_list[7], 71), 0)
    neighbours = draw_neighbours(jax.random.fold_in(key_list[7], 71), 0)
    counts = draw_counts(jax.random.fold_in(key_list[7], 71), 0)
    return {"features": features, "w_qkv": w_qkv, "w_out": w_out, "bias_gain": bias_gain, "edge_bias": edge_bias, "neighbours": neighbours, "counts": counts}


def reference(features, w_qkv, w_out, bias_gain, edge_bias, neighbours, counts):
    queries = jnp.dot(features, w_qkv[0], preferred_element_type=jnp.float32).astype(jnp.bfloat16)
    keys = jnp.dot(features, w_qkv[1], preferred_element_type=jnp.float32).astype(jnp.bfloat16)
    values = jnp.dot(features, w_qkv[2], preferred_element_type=jnp.float32).astype(jnp.bfloat16)
    query_blocks = queries.reshape(QBLOCKS, BLK, HEADS, HD)
    key_blocks = keys.reshape(QBLOCKS, BLK, HEADS, HD)
    value_blocks = values.reshape(QBLOCKS, BLK, HEADS, HD)
    scale = HD ** -0.5

    def one_block(inputs):
        query_tile, slot_ids, live_count, bias_tile = inputs
        near_keys = key_blocks[slot_ids].astype(jnp.float32)
        near_values = value_blocks[slot_ids].astype(jnp.float32)
        score = jnp.einsum("qhd,nkhd->hqnk", query_tile.astype(jnp.float32), near_keys) * scale
        bias_terms = bias_tile.astype(jnp.float32).reshape(BLK, NB, BLK)
        score = score + bias_gain[:, None, None, None] * bias_terms[None]
        live = jnp.arange(NB, dtype=jnp.int32) < live_count
        score = jnp.where(live[None, None, :, None], score, jnp.float32(-1e30))
        top = jnp.max(score, axis=(2, 3), keepdims=True)
        expo = jnp.exp(score - top)
        total = jnp.sum(expo, axis=(2, 3), keepdims=True)
        weights = (expo / total).astype(jnp.bfloat16)
        result = jnp.einsum("hqnk,nkhd->qhd", weights.astype(jnp.float32), near_values)
        return result.astype(jnp.bfloat16).reshape(BLK, HEADS * HD)

    attended = lax.map(one_block, (query_blocks, neighbours, counts, edge_bias))
    attended = attended.reshape(NODES, HEADS * HD)
    return jnp.dot(attended, w_out, preferred_element_type=jnp.float32).astype(jnp.bfloat16)
```

```python
import jax
import jax.numpy as jnp
from jax import lax
from jax.experimental import pallas as pl
from jax.experimental.pallas import tpu as pltpu
from jax.sharding import PartitionSpec as P

HD = 64
BLK = 64
NB = 64


def _attend_kernel(nbr_ref, cnt_ref, gain_ref, q_ref, bias_ref, kv_hbm, o_ref, kv_buf, sem):
    g = pl.program_id(0)
    steps = pl.num_programs(0)
    width = kv_buf.shape[-1]
    half_w = width // 2
    pairs = half_w // 128

    def start(gi, slot):
        def issue(j, carry):
            pltpu.make_async_copy(
                kv_hbm.at[nbr_ref[gi, j]], kv_buf.at[slot, j], sem.at[slot]
            ).start()
            return carry

        lax.fori_loop(0, NB, issue, 0)

    @pl.when(g == 0)
    def _():
        start(0, 0)

    @pl.when(g + 1 < steps)
    def _():
        start(g + 1, (g + 1) % 2)

    slot = g % 2
    pltpu.make_async_copy(kv_hbm.at[pl.ds(0, NB)], kv_buf.at[slot], sem.at[slot]).wait()

    span = NB * BLK
    live_cols = cnt_ref[g] * BLK
    col = lax.broadcasted_iota(jnp.int32, (BLK, span), 1)
    live = col < live_cols
    bias = bias_ref[0].astype(jnp.float32)
    q = q_ref[0]
    lane = lax.broadcasted_iota(jnp.int32, (BLK, 128), 1)
    scale = HD ** (-0.5)
    outs = []
    for pair in range(pairs):
        kp = kv_buf[slot, :, :, pair * 128:(pair + 1) * 128].reshape(span, 128)
        vp = kv_buf[slot, :, :, half_w + pair * 128:half_w + (pair + 1) * 128].reshape(span, 128)
        qp = q[:, pair * 128:(pair + 1) * 128]
        res = None
        for half in range(2):
            h = pair * 2 + half
            in_head = (lane >= half * HD) & (lane < (half + 1) * HD)
            qm = jnp.where(in_head, qp, jnp.zeros_like(qp))
            s = lax.dot_general(
                qm, kp, (((1,), (1,)), ((), ())), preferred_element_type=jnp.float32
            )
            s = s * scale + gain_ref[h] * bias
            s = jnp.where(live, s, jnp.float32(-1e30))
            top = jnp.max(s, axis=1, keepdims=True)
            expo = jnp.exp(s - top)
            total = jnp.sum(expo, axis=1, keepdims=True)
            w = (expo * (1.0 / total)).astype(jnp.bfloat16)
            o = jnp.dot(w, vp, preferred_element_type=jnp.float32)
            res = o if res is None else jnp.where(lane < HD, res, o)
        outs.append(res.astype(jnp.bfloat16))
    o_ref[0] = jnp.concatenate(outs, axis=1)


def attend(nbr, cnt, gain, q_blocks, bias, kv_table):
    blocks, _, width_q = q_blocks.shape
    width = kv_table.shape[-1]
    span = NB * BLK
    grid_spec = pltpu.PrefetchScalarGridSpec(
        num_scalar_prefetch=2,
        grid=(blocks,),
        in_specs=[
            pl.BlockSpec(memory_space=pltpu.SMEM),
            pl.BlockSpec((1, BLK, width_q), lambda g, n, c: (g, 0, 0)),
            pl.BlockSpec((1, BLK, span), lambda g, n, c: (g, 0, 0)),
            pl.BlockSpec(memory_space=pl.ANY),
        ],
        out_specs=pl.BlockSpec((1, BLK, width_q), lambda g, n, c: (g, 0, 0)),
        scratch_shapes=[
            pltpu.VMEM((2, NB, BLK, width), jnp.bfloat16),
            pltpu.SemaphoreType.DMA((2,)),
        ],
    )
    return pl.pallas_call(
        _attend_kernel,
        grid_spec=grid_spec,
        out_shape=jax.ShapeDtypeStruct((blocks, BLK, width_q), jnp.bfloat16),
        compiler_params=pltpu.CompilerParams(
            dimension_semantics=("arbitrary",), vmem_limit_bytes=48 * 1024 * 1024
        ),
    )(nbr, cnt, gain, q_blocks, bias, kv_table)


def body(features, w_qkv, w_out, bias_gain, edge_bias, neighbours, counts):
    rows = features.shape[0]
    width_heads = w_qkv.shape[2]
    blocks_dev = rows // BLK
    queries = jnp.dot(features, w_qkv[0], preferred_element_type=jnp.float32).astype(jnp.bfloat16)
    keys = jnp.dot(features, w_qkv[1], preferred_element_type=jnp.float32).astype(jnp.bfloat16)
    values = jnp.dot(features, w_qkv[2], preferred_element_type=jnp.float32).astype(jnp.bfloat16)
    kv = jnp.concatenate([keys, values], axis=1)
    gathered = lax.all_gather(kv, "row", axis=0, tiled=True)
    kv_table = gathered.reshape(-1, BLK, 2 * width_heads)
    w_cols = lax.all_to_all(w_out, "head", 1, 0, tiled=True)
    attended = attend(
        neighbours,
        counts,
        bias_gain,
        queries.reshape(blocks_dev, BLK, width_heads),
        edge_bias,
        kv_table,
    ).reshape(rows, width_heads)
    attended_all = lax.all_gather(attended, "head", axis=1, tiled=True)
    return jnp.dot(attended_all, w_cols, preferred_element_type=jnp.float32).astype(jnp.bfloat16)


def solution(mesh):
    in_specs = (
        P("row", None),
        P(None, None, "head"),
        P("head", None),
        P("head"),
        P("row", None, None),
        P("row", None),
        P("row"),
    )
    out_specs = P("row", "head")
    return jax.shard_map(body, mesh=mesh, in_specs=in_specs, out_specs=out_specs, check_vma=False)
```

```python
import jax
import jax.numpy as jnp
from jax import lax
from jax.experimental import pallas as pl
from jax.experimental.pallas import tpu as pltpu
from jax.sharding import PartitionSpec as P

HD = 64
BLK = 64
NB = 64


def _attend_kernel(nbr_ref, cnt_ref, gain_ref, q_ref, bias_ref, kv_hbm, o_ref, kv_buf, sem):
    g = pl.program_id(0)
    steps = pl.num_programs(0)
    width = kv_buf.shape[-1]
    half_w = width // 2
    pairs = half_w // 128

    def start(gi, slot):
        def issue(j, carry):
            pltpu.make_async_copy(
                kv_hbm.at[nbr_ref[gi, j]], kv_buf.at[slot, j], sem.at[slot]
            ).start()
            return carry

        lax.fori_loop(0, NB, issue, 0)

    @pl.when(g == 0)
    def _():
        start(0, 0)

    @pl.when(g + 1 < steps)
    def _():
        start(g + 1, (g + 1) % 2)

    slot = g % 2
    pltpu.make_async_copy(kv_hbm.at[pl.ds(0, NB)], kv_buf.at[slot], sem.at[slot]).wait()

    span = NB * BLK
    live_cols = cnt_ref[g] * BLK
    col = lax.broadcasted_iota(jnp.int32, (BLK, span), 1)
    live = col < live_cols
    bias = bias_ref[0].astype(jnp.float32)
    q = q_ref[0]
    lane = lax.broadcasted_iota(jnp.int32, (BLK, 128), 1)
    scale = HD ** (-0.5)
    outs = []
    for pair in range(pairs):
        kp = kv_buf[slot, :, :, pair * 128:(pair + 1) * 128].reshape(span, 128)
        vp = kv_buf[slot, :, :, half_w + pair * 128:half_w + (pair + 1) * 128].reshape(span, 128)
        qp = q[:, pair * 128:(pair + 1) * 128]
        res = None
        for half in range(2):
            h = pair * 2 + half
            in_head = (lane >= half * HD) & (lane < (half + 1) * HD)
            qm = jnp.where(in_head, qp, jnp.zeros_like(qp))
            s = lax.dot_general(
                qm, kp, (((1,), (1,)), ((), ())), preferred_element_type=jnp.float32
            )
            s = s * scale + gain_ref[h] * bias
            s = jnp.where(live, s, jnp.float32(-1e30))
            top = jnp.max(s, axis=1, keepdims=True)
            expo = jnp.exp(s - top)
            total = jnp.sum(expo, axis=1, keepdims=True)
            w = (expo * (1.0 / total)).astype(jnp.bfloat16)
            o = jnp.dot(w, vp, preferred_element_type=jnp.float32)
            res = o if res is None else jnp.where(lane < HD, res, o)
        outs.append(res.astype(jnp.bfloat16))
    o_ref[0] = jnp.concatenate(outs, axis=1)


def attend(nbr, cnt, gain, q_blocks, bias, kv_table):
    blocks, _, width_q = q_blocks.shape
    width = kv_table.shape[-1]
    span = NB * BLK
    grid_spec = pltpu.PrefetchScalarGridSpec(
        num_scalar_prefetch=2,
        grid=(blocks,),
        in_specs=[
            pl.BlockSpec(memory_space=pltpu.SMEM),
            pl.BlockSpec((1, BLK, width_q), lambda g, n, c: (g, 0, 0)),
            pl.BlockSpec((1, BLK, span), lambda g, n, c: (g, 0, 0)),
            pl.BlockSpec(memory_space=pl.ANY),
        ],
        out_specs=pl.BlockSpec((1, BLK, width_q), lambda g, n, c: (g, 0, 0)),
        scratch_shapes=[
            pltpu.VMEM((2, NB, BLK, width), jnp.bfloat16),
            pltpu.SemaphoreType.DMA((2,)),
        ],
    )
    return pl.pallas_call(
        _attend_kernel,
        grid_spec=grid_spec,
        out_shape=jax.ShapeDtypeStruct((blocks, BLK, width_q), jnp.bfloat16),
        compiler_params=pltpu.CompilerParams(
            dimension_semantics=("arbitrary",), vmem_limit_bytes=48 * 1024 * 1024
        ),
    )(nbr, cnt, gain, q_blocks, bias, kv_table)


def body(features, w_qkv, w_out, bias_gain, edge_bias, neighbours, counts):
    rows = features.shape[0]
    width_heads = w_qkv.shape[2]
    blocks_dev = rows // BLK
    head_devs = lax.axis_size("head")
    me = lax.axis_index("head")
    chunk = 128
    chunks = width_heads // chunk
    queries = jnp.dot(features, w_qkv[0], preferred_element_type=jnp.float32).astype(jnp.bfloat16)
    keys = jnp.dot(features, w_qkv[1], preferred_element_type=jnp.float32).astype(jnp.bfloat16)
    values = jnp.dot(features, w_qkv[2], preferred_element_type=jnp.float32).astype(jnp.bfloat16)
    w_parts = []
    for s in range(1, head_devs):
        target = (me + s) % head_devs
        piece = lax.dynamic_slice_in_dim(w_out, target * width_heads, width_heads, axis=1)
        perm = [(i, (i + s) % head_devs) for i in range(head_devs)]
        w_parts.append(lax.ppermute(piece, "head", perm))
    w_own = lax.dynamic_slice_in_dim(w_out, me * width_heads, width_heads, axis=1)
    outs = []
    for c in range(chunks):
        cols = slice(c * chunk, (c + 1) * chunk)
        kv = jnp.concatenate([keys[:, cols], values[:, cols]], axis=1)
        kv = kv.reshape(blocks_dev, BLK, 2 * chunk)
        kv_table = lax.all_gather(kv, "row", axis=0, tiled=True)
        outs.append(
            attend(
                neighbours,
                counts,
                bias_gain[c * 2:(c + 1) * 2],
                queries[:, cols].reshape(blocks_dev, BLK, chunk),
                edge_bias,
                kv_table,
            ).reshape(rows, chunk)
        )
    attended = jnp.concatenate(outs, axis=1)
    total = jnp.dot(attended, w_own, preferred_element_type=jnp.float32)
    for s in range(1, head_devs):
        perm = [(i, (i + s) % head_devs) for i in range(head_devs)]
        att_s = lax.ppermute(attended, "head", perm)
        total = total + jnp.dot(att_s, w_parts[s - 1], preferred_element_type=jnp.float32)
    return total.astype(jnp.bfloat16)


def solution(mesh):
    in_specs = (
        P("row", None),
        P(None, None, "head"),
        P("head", None),
        P("head"),
        P("row", None, None),
        P("row", None),
        P("row"),
    )
    out_specs = P("row", "head")
    return jax.shard_map(body, mesh=mesh, in_specs=in_specs, out_specs=out_specs, check_vma=False)
```

```python
import jax
import jax.numpy as jnp
from jax import lax
from jax.experimental import pallas as pl
from jax.experimental.pallas import tpu as pltpu
from jax.sharding import PartitionSpec as P

HD = 64
BLK = 64
NB = 64


def _attend_kernel(nbr_ref, cnt_ref, gain_ref, q_ref, bias_ref, kv_hbm, o_ref, kv_buf, sem):
    g = pl.program_id(0)
    steps = pl.num_programs(0)
    width = kv_buf.shape[-1]
    half_w = width // 2
    pairs = half_w // 128

    def start(gi, slot):
        def issue(j, carry):
            pltpu.make_async_copy(
                kv_hbm.at[nbr_ref[gi, j]], kv_buf.at[slot, j], sem.at[slot]
            ).start()
            return carry

        lax.fori_loop(0, NB, issue, 0)

    @pl.when(g == 0)
    def _():
        start(0, 0)

    @pl.when(g + 1 < steps)
    def _():
        start(g + 1, (g + 1) % 2)

    slot = g % 2
    pltpu.make_async_copy(kv_hbm.at[pl.ds(0, NB)], kv_buf.at[slot], sem.at[slot]).wait()

    span = NB * BLK
    live_cols = cnt_ref[g] * BLK
    col = lax.broadcasted_iota(jnp.int32, (BLK, span), 1)
    live = col < live_cols
    bias = bias_ref[0].astype(jnp.float32)
    q = q_ref[0]
    lane = lax.broadcasted_iota(jnp.int32, (BLK, 128), 1)
    scale = HD ** (-0.5)
    outs = []
    for pair in range(pairs):
        kp = kv_buf[slot, :, :, pair * 128:(pair + 1) * 128].reshape(span, 128)
        vp = kv_buf[slot, :, :, half_w + pair * 128:half_w + (pair + 1) * 128].reshape(span, 128)
        qp = q[:, pair * 128:(pair + 1) * 128]
        res = None
        for half in range(2):
            h = pair * 2 + half
            in_head = (lane >= half * HD) & (lane < (half + 1) * HD)
            qm = jnp.where(in_head, qp, jnp.zeros_like(qp))
            s = lax.dot_general(
                qm, kp, (((1,), (1,)), ((), ())), preferred_element_type=jnp.float32
            )
            s = s * scale + gain_ref[h] * bias
            s = jnp.where(live, s, jnp.float32(-1e30))
            top = jnp.max(s, axis=1, keepdims=True)
            expo = jnp.exp(s - top)
            total = jnp.sum(expo, axis=1, keepdims=True)
            w = (expo * (1.0 / total)).astype(jnp.bfloat16)
            o = jnp.dot(w, vp, preferred_element_type=jnp.float32)
            res = o if res is None else jnp.where(lane < HD, res, o)
        outs.append(res.astype(jnp.bfloat16))
    o_ref[0] = jnp.concatenate(outs, axis=1)


def attend(nbr, cnt, gain, q_blocks, bias, kv_table):
    blocks, _, width_q = q_blocks.shape
    width = kv_table.shape[-1]
    span = NB * BLK
    grid_spec = pltpu.PrefetchScalarGridSpec(
        num_scalar_prefetch=2,
        grid=(blocks,),
        in_specs=[
            pl.BlockSpec(memory_space=pltpu.SMEM),
            pl.BlockSpec((1, BLK, width_q), lambda g, n, c: (g, 0, 0)),
            pl.BlockSpec((1, BLK, span), lambda g, n, c: (g, 0, 0)),
            pl.BlockSpec(memory_space=pl.ANY),
        ],
        out_specs=pl.BlockSpec((1, BLK, width_q), lambda g, n, c: (g, 0, 0)),
        scratch_shapes=[
            pltpu.VMEM((2, NB, BLK, width), jnp.bfloat16),
            pltpu.SemaphoreType.DMA((2,)),
        ],
    )
    return pl.pallas_call(
        _attend_kernel,
        grid_spec=grid_spec,
        out_shape=jax.ShapeDtypeStruct((blocks, BLK, width_q), jnp.bfloat16),
        compiler_params=pltpu.CompilerParams(
            dimension_semantics=("arbitrary",), vmem_limit_bytes=48 * 1024 * 1024
        ),
    )(nbr, cnt, gain, q_blocks, bias, kv_table)


def plan_requests(neighbours, per_owner, owners):
    owner = neighbours // per_owner
    local = neighbours % per_owner
    flat = neighbours.reshape(-1)
    ids = jnp.arange(owners * per_owner, dtype=jnp.int32)
    present = jnp.any(flat[:, None] == ids[None, :], axis=0).reshape(owners, per_owner)
    lidx = jnp.arange(per_owner, dtype=jnp.int32)[None, :]
    first = jnp.min(jnp.where(present, lidx, per_owner), axis=1)
    first = jnp.where(first == per_owner, 0, first)
    second = jnp.max(jnp.where(present, lidx, -1), axis=1)
    second = jnp.where(second < 0, first, second)
    req = jnp.stack([first, second], axis=1).astype(jnp.int32)
    pos = owner * 2 + (local != first[owner]).astype(jnp.int32)
    return req, pos.astype(jnp.int32)


def body(features, w_qkv, w_out, bias_gain, edge_bias, neighbours, counts):
    rows = features.shape[0]
    width_heads = w_qkv.shape[2]
    blocks_dev = rows // BLK
    head_devs = lax.axis_size("head")
    row_devs = lax.axis_size("row")
    me = lax.axis_index("head")
    req, pos = plan_requests(neighbours, blocks_dev, row_devs)
    wanted = lax.all_to_all(req, "row", 0, 0, tiled=True)
    queries = jnp.dot(features, w_qkv[0], preferred_element_type=jnp.float32).astype(jnp.bfloat16)
    keys = jnp.dot(features, w_qkv[1], preferred_element_type=jnp.float32).astype(jnp.bfloat16)
    values = jnp.dot(features, w_qkv[2], preferred_element_type=jnp.float32).astype(jnp.bfloat16)
    kv = jnp.concatenate([keys, values], axis=1).reshape(blocks_dev, BLK, 2 * width_heads)
    outgoing = jnp.take(kv, wanted.reshape(-1), axis=0)
    kv_table = lax.all_to_all(outgoing, "row", 0, 0, tiled=True)
    w_parts = []
    for s in range(1, head_devs):
        target = (me + s) % head_devs
        piece = lax.dynamic_slice_in_dim(w_out, target * width_heads, width_heads, axis=1)
        perm = [(i, (i + s) % head_devs) for i in range(head_devs)]
        w_parts.append(lax.ppermute(piece, "head", perm))
    w_own = lax.dynamic_slice_in_dim(w_out, me * width_heads, width_heads, axis=1)
    attended = attend(
        pos,
        counts,
        bias_gain,
        queries.reshape(blocks_dev, BLK, width_heads),
        edge_bias,
        kv_table,
    ).reshape(rows, width_heads)
    total = jnp.dot(attended, w_own, preferred_element_type=jnp.float32)
    for s in range(1, head_devs):
        perm = [(i, (i + s) % head_devs) for i in range(head_devs)]
        att_s = lax.ppermute(attended, "head", perm)
        total = total + jnp.dot(att_s, w_parts[s - 1], preferred_element_type=jnp.float32)
    return total.astype(jnp.bfloat16)


def solution(mesh):
    in_specs = (
        P("row", None),
        P(None, None, "head"),
        P("head", None),
        P("head"),
        P("row", None, None),
        P("row", None),
        P("row"),
    )
    out_specs = P("row", "head")
    return jax.shard_map(body, mesh=mesh, in_specs=in_specs, out_specs=out_specs, check_vma=False)
```

```python
import jax
import jax.numpy as jnp
from jax import lax
from jax.experimental import pallas as pl
from jax.experimental.pallas import tpu as pltpu
from jax.sharding import PartitionSpec as P

HD = 64
BLK = 64
NB = 64


def _attend_kernel(nbr_ref, cnt_ref, gain_ref, q_ref, bias_ref, kv_hbm, o_ref, kv_buf, sem):
    g = pl.program_id(0)
    steps = pl.num_programs(0)
    width = kv_buf.shape[-1]
    half_w = width // 2
    pairs = half_w // 128

    def start(gi, slot):
        def issue(j, carry):
            pltpu.make_async_copy(
                kv_hbm.at[nbr_ref[gi, j]], kv_buf.at[slot, j], sem.at[slot]
            ).start()
            return carry

        lax.fori_loop(0, NB, issue, 0)

    @pl.when(g == 0)
    def _():
        start(0, 0)

    @pl.when(g + 1 < steps)
    def _():
        start(g + 1, (g + 1) % 2)

    slot = g % 2
    pltpu.make_async_copy(kv_hbm.at[pl.ds(0, NB)], kv_buf.at[slot], sem.at[slot]).wait()

    span = NB * BLK
    live_cols = cnt_ref[g] * BLK
    col = lax.broadcasted_iota(jnp.int32, (BLK, span), 1)
    live = col < live_cols
    bias = bias_ref[0].astype(jnp.float32)
    q = q_ref[0]
    lane = lax.broadcasted_iota(jnp.int32, (BLK, 128), 1)
    scale = HD ** (-0.5)
    outs = []
    for pair in range(pairs):
        kp = kv_buf[slot, :, :, pair * 128:(pair + 1) * 128].reshape(span, 128)
        vp = kv_buf[slot, :, :, half_w + pair * 128:half_w + (pair + 1) * 128].reshape(span, 128)
        qp = q[:, pair * 128:(pair + 1) * 128]
        res = None
        for half in range(2):
            h = pair * 2 + half
            in_head = (lane >= half * HD) & (lane < (half + 1) * HD)
            qm = jnp.where(in_head, qp, jnp.zeros_like(qp))
            s = lax.dot_general(
                qm, kp, (((1,), (1,)), ((), ())), preferred_element_type=jnp.float32
            )
            s = s * scale + gain_ref[h] * bias
            s = jnp.where(live, s, jnp.float32(-1e30))
            top = jnp.max(s, axis=1, keepdims=True)
            expo = jnp.exp(s - top)
            total = jnp.sum(expo, axis=1, keepdims=True)
            w = (expo * (1.0 / total)).astype(jnp.bfloat16)
            o = jnp.dot(w, vp, preferred_element_type=jnp.float32)
            res = o if res is None else jnp.where(lane < HD, res, o)
        outs.append(res.astype(jnp.bfloat16))
    o_ref[0] = jnp.concatenate(outs, axis=1)


def attend(nbr, cnt, gain, q_blocks, bias, kv_table):
    blocks, _, width_q = q_blocks.shape
    width = kv_table.shape[-1]
    span = NB * BLK
    grid_spec = pltpu.PrefetchScalarGridSpec(
        num_scalar_prefetch=2,
        grid=(blocks,),
        in_specs=[
            pl.BlockSpec(memory_space=pltpu.SMEM),
            pl.BlockSpec((1, BLK, width_q), lambda g, n, c: (g, 0, 0)),
            pl.BlockSpec((1, BLK, span), lambda g, n, c: (g, 0, 0)),
            pl.BlockSpec(memory_space=pl.ANY),
        ],
        out_specs=pl.BlockSpec((1, BLK, width_q), lambda g, n, c: (g, 0, 0)),
        scratch_shapes=[
            pltpu.VMEM((2, NB, BLK, width), jnp.bfloat16),
            pltpu.SemaphoreType.DMA((2,)),
        ],
    )
    return pl.pallas_call(
        _attend_kernel,
        grid_spec=grid_spec,
        out_shape=jax.ShapeDtypeStruct((blocks, BLK, width_q), jnp.bfloat16),
        compiler_params=pltpu.CompilerParams(
            dimension_semantics=("arbitrary",), vmem_limit_bytes=48 * 1024 * 1024
        ),
    )(nbr, cnt, gain, q_blocks, bias, kv_table)


def plan_requests(neighbours, per_owner, owners):
    owner = neighbours // per_owner
    local = neighbours % per_owner
    flat = neighbours.reshape(-1)
    ids = jnp.arange(owners * per_owner, dtype=jnp.int32)
    present = jnp.any(flat[:, None] == ids[None, :], axis=0).reshape(owners, per_owner)
    lidx = jnp.arange(per_owner, dtype=jnp.int32)[None, :]
    first = jnp.min(jnp.where(present, lidx, per_owner), axis=1)
    first = jnp.where(first == per_owner, 0, first)
    second = jnp.max(jnp.where(present, lidx, -1), axis=1)
    second = jnp.where(second < 0, first, second)
    req = jnp.stack([first, second], axis=1).astype(jnp.int32)
    pos = owner * 2 + (local != first[owner]).astype(jnp.int32)
    return req, pos.astype(jnp.int32)


def body(features, w_qkv, w_out, bias_gain, edge_bias, neighbours, counts):
    rows = features.shape[0]
    width_heads = w_qkv.shape[2]
    blocks_dev = rows // BLK
    head_devs = lax.axis_size("head")
    row_devs = lax.axis_size("row")
    me = lax.axis_index("head")
    chunk = 128
    chunks = width_heads // chunk
    req, pos = plan_requests(neighbours, blocks_dev, row_devs)
    wanted = lax.all_to_all(req, "row", 0, 0, tiled=True).reshape(-1)
    queries = jnp.dot(features, w_qkv[0], preferred_element_type=jnp.float32).astype(jnp.bfloat16)
    keys = jnp.dot(features, w_qkv[1], preferred_element_type=jnp.float32).astype(jnp.bfloat16)
    values = jnp.dot(features, w_qkv[2], preferred_element_type=jnp.float32).astype(jnp.bfloat16)
    w_parts = []
    for s in range(1, head_devs):
        target = (me + s) % head_devs
        piece = lax.dynamic_slice_in_dim(w_out, target * width_heads, width_heads, axis=1)
        perm = [(i, (i + s) % head_devs) for i in range(head_devs)]
        w_parts.append(lax.ppermute(piece, "head", perm))
    w_own = lax.dynamic_slice_in_dim(w_out, me * width_heads, width_heads, axis=1)
    outgoing = []
    for c in range(chunks):
        cols = slice(c * chunk, (c + 1) * chunk)
        kv = jnp.concatenate([keys[:, cols], values[:, cols]], axis=1)
        kv = kv.reshape(blocks_dev, BLK, 2 * chunk)
        outgoing.append(jnp.take(kv, wanted, axis=0, mode="clip"))
    total = None
    table = None
    for c in range(chunks):
        cols = slice(c * chunk, (c + 1) * chunk)
        send = outgoing[c]
        if table is not None:
            table, send = lax.optimization_barrier((table, send))
        table = lax.all_to_all(send, "row", 0, 0, tiled=True)
        att = attend(
            pos,
            counts,
            bias_gain[c * 2:(c + 1) * 2],
            queries[:, cols].reshape(blocks_dev, BLK, chunk),
            edge_bias,
            table,
        ).reshape(rows, chunk)
        part = jnp.dot(att, w_own[cols], preferred_element_type=jnp.float32)
        total = part if total is None else total + part
        for s in range(1, head_devs):
            perm = [(i, (i + s) % head_devs) for i in range(head_devs)]
            att_s = lax.ppermute(att, "head", perm)
            total = total + jnp.dot(att_s, w_parts[s - 1][cols], preferred_element_type=jnp.float32)
    return total.astype(jnp.bfloat16)


def solution(mesh):
    in_specs = (
        P("row", None),
        P(None, None, "head"),
        P("head", None),
        P("head"),
        P("row", None, None),
        P("row", None),
        P("row"),
    )
    out_specs = P("row", "head")
    return jax.shard_map(body, mesh=mesh, in_specs=in_specs, out_specs=out_specs, check_vma=False)
```

```python
import functools

import jax
import jax.numpy as jnp
from jax import lax
from jax.experimental import pallas as pl
from jax.experimental.pallas import tpu as pltpu
from jax.sharding import PartitionSpec as P

HD = 64
BLK = 64
NB = 64


CH = 8


def _attend_kernel(g0, nbr_ref, cnt_ref, gain_ref, q_ref, bias_ref, kv_hbm, o_ref,
                   kv_buf, s_scr, bm_scr, sem):
    g = pl.program_id(0)
    steps = pl.num_programs(0)
    width = kv_buf.shape[-1]
    half_w = width // 2
    pairs = half_w // 128
    span = NB * BLK
    cw = CH * BLK
    nchunks = NB // CH

    def live_chunks(gi):
        return (cnt_ref[g0 + gi] + (CH - 1)) // CH

    def start(gi, slot):
        def issue(c, carry):
            for i in range(CH):
                j = c * CH + i
                pltpu.make_async_copy(
                    kv_hbm.at[nbr_ref[g0 + gi, j]], kv_buf.at[slot, j], sem.at[slot, c]
                ).start()
            return carry

        lax.fori_loop(0, live_chunks(gi), issue, 0)

    @pl.when(g == 0)
    def _():
        start(0, 0)

    @pl.when(g + 1 < steps)
    def _():
        start(g + 1, (g + 1) % 2)

    slot = g % 2
    nc = live_chunks(g)

    def wait(c, carry):
        pltpu.make_async_copy(
            kv_hbm.at[pl.ds(0, CH)], kv_buf.at[slot, pl.ds(c * CH, CH)], sem.at[slot, c]
        ).wait()
        return carry

    lax.fori_loop(0, nc, wait, 0)

    live_cols = cnt_ref[g0 + g] * BLK
    col = lax.broadcasted_iota(jnp.int32, (BLK, cw), 1)
    for c in range(nchunks):
        @pl.when(c < nc)
        def _():
            b = bias_ref[0, :, c * cw:(c + 1) * cw].astype(jnp.float32)
            bm_scr[c] = jnp.where(col + c * cw < live_cols, b, -jnp.inf)

    q = q_ref[0]
    lane = lax.broadcasted_iota(jnp.int32, (BLK, 128), 1)
    scale = HD ** (-0.5)
    outs = []
    for pair in range(pairs):
        qp = (q[:, pair * 128:(pair + 1) * 128].astype(jnp.float32) * scale).astype(jnp.bfloat16)
        k_lo = pair * 128
        v_lo = half_w + pair * 128
        res = None
        for half in range(2):
            h = pair * 2 + half
            in_head = (lane >= half * HD) & (lane < (half + 1) * HD)
            qm = jnp.where(in_head, qp, jnp.zeros_like(qp))
            gain = gain_ref[h]

            def score(c, top):
                kc = kv_buf[slot, pl.ds(c * CH, CH), :, k_lo:k_lo + 128].reshape(cw, 128)
                s = lax.dot_general(
                    qm, kc, (((1,), (1,)), ((), ())), preferred_element_type=jnp.float32
                )
                s = s + gain * bm_scr[c]
                s_scr[c] = s
                return jnp.maximum(top, jnp.max(s, axis=1, keepdims=True))

            top = lax.fori_loop(0, nc, score, jnp.full((BLK, 1), -jnp.inf, jnp.float32))

            def accumulate(c, carry):
                total, acc = carry
                expo = jnp.exp(s_scr[c] - top)
                total = total + jnp.sum(expo, axis=1, keepdims=True)
                vc = kv_buf[slot, pl.ds(c * CH, CH), :, v_lo:v_lo + 128].reshape(cw, 128)
                acc = acc + jnp.dot(expo.astype(jnp.bfloat16), vc, preferred_element_type=jnp.float32)
                return total, acc

            total, acc = lax.fori_loop(
                0, nc, accumulate,
                (jnp.zeros((BLK, 1), jnp.float32), jnp.zeros((BLK, 128), jnp.float32)),
            )
            o = acc * (1.0 / total)
            res = o if res is None else jnp.where(lane < HD, res, o)
        outs.append(res.astype(jnp.bfloat16))
    o_ref[0] = jnp.concatenate(outs, axis=1)


def attend(nbr, cnt, gain, q_blocks, bias, kv_table, g0, steps):
    width_q = q_blocks.shape[-1]
    width = kv_table.shape[-1]
    span = NB * BLK
    grid_spec = pltpu.PrefetchScalarGridSpec(
        num_scalar_prefetch=2,
        grid=(steps,),
        in_specs=[
            pl.BlockSpec(memory_space=pltpu.SMEM),
            pl.BlockSpec((1, BLK, width_q), lambda g, n, c: (g + g0, 0, 0)),
            pl.BlockSpec((1, BLK, span), lambda g, n, c: (g + g0, 0, 0)),
            pl.BlockSpec(memory_space=pl.ANY),
        ],
        out_specs=pl.BlockSpec((1, BLK, width_q), lambda g, n, c: (g, 0, 0)),
        scratch_shapes=[
            pltpu.VMEM((2, NB, BLK, width), jnp.bfloat16),
            pltpu.VMEM((NB // CH, BLK, CH * BLK), jnp.float32),
            pltpu.VMEM((NB // CH, BLK, CH * BLK), jnp.float32),
            pltpu.SemaphoreType.DMA((2, NB // CH)),
        ],
    )
    return pl.pallas_call(
        functools.partial(_attend_kernel, g0),
        grid_spec=grid_spec,
        out_shape=jax.ShapeDtypeStruct((steps, BLK, width_q), jnp.bfloat16),
        compiler_params=pltpu.CompilerParams(
            dimension_semantics=("arbitrary",), vmem_limit_bytes=48 * 1024 * 1024
        ),
    )(nbr, cnt, gain, q_blocks, bias, kv_table)


def plan_requests(neighbours, per_owner, owners):
    owner = neighbours // per_owner
    local = neighbours % per_owner
    flat = neighbours.reshape(-1)
    ids = jnp.arange(owners * per_owner, dtype=jnp.int32)
    present = jnp.any(flat[:, None] == ids[None, :], axis=0).reshape(owners, per_owner)
    lidx = jnp.arange(per_owner, dtype=jnp.int32)[None, :]
    first = jnp.min(jnp.where(present, lidx, per_owner), axis=1)
    first = jnp.where(first == per_owner, 0, first)
    second = jnp.max(jnp.where(present, lidx, -1), axis=1)
    second = jnp.where(second < 0, first, second)
    req = jnp.stack([first, second], axis=1).astype(jnp.int32)
    pos = owner * 2 + (local != first[owner]).astype(jnp.int32)
    return req, pos.astype(jnp.int32)


def body(features, w_qkv, w_out, bias_gain, edge_bias, neighbours, counts):
    rows = features.shape[0]
    width_heads = w_qkv.shape[2]
    blocks_dev = rows // BLK
    head_devs = lax.axis_size("head")
    row_devs = lax.axis_size("row")
    me = lax.axis_index("head")
    req, pos = plan_requests(neighbours, blocks_dev, row_devs)
    wanted = lax.all_to_all(req, "row", 0, 0, tiled=True).reshape(-1)
    queries = jnp.dot(features, w_qkv[0], preferred_element_type=jnp.float32).astype(jnp.bfloat16)
    keys = jnp.dot(features, w_qkv[1], preferred_element_type=jnp.float32).astype(jnp.bfloat16)
    values = jnp.dot(features, w_qkv[2], preferred_element_type=jnp.float32).astype(jnp.bfloat16)
    kv = jnp.concatenate([keys, values], axis=1).reshape(blocks_dev, BLK, 2 * width_heads)
    outgoing = jnp.take(kv, wanted, axis=0, mode="clip")
    kv_table = lax.all_to_all(outgoing, "row", 0, 0, tiled=True)
    w_parts = []
    for s in range(1, head_devs):
        target = (me + s) % head_devs
        piece = lax.dynamic_slice_in_dim(w_out, target * width_heads, width_heads, axis=1)
        perm = [(i, (i + s) % head_devs) for i in range(head_devs)]
        w_parts.append(lax.ppermute(piece, "head", perm))
    w_own = lax.dynamic_slice_in_dim(w_out, me * width_heads, width_heads, axis=1)
    q_blocks = queries.reshape(blocks_dev, BLK, width_heads)
    halves = 2
    steps = blocks_dev // halves
    results = []
    for part in range(halves):
        att = attend(pos, counts, bias_gain, q_blocks, edge_bias, kv_table, part * steps, steps)
        att = att.reshape(steps * BLK, width_heads)
        total = jnp.dot(att, w_own, preferred_element_type=jnp.float32)
        for s in range(1, head_devs):
            perm = [(i, (i + s) % head_devs) for i in range(head_devs)]
            att_s = lax.ppermute(att, "head", perm)
            total = total + jnp.dot(att_s, w_parts[s - 1], preferred_element_type=jnp.float32)
        results.append(total.astype(jnp.bfloat16))
    return jnp.concatenate(results, axis=0)


def solution(mesh):
    in_specs = (
        P("row", None),
        P(None, None, "head"),
        P("head", None),
        P("head"),
        P("row", None, None),
        P("row", None),
        P("row"),
    )
    out_specs = P("row", "head")
    return jax.shard_map(body, mesh=mesh, in_specs=in_specs, out_specs=out_specs, check_vma=False)
```

```python
import functools

import jax
import jax.numpy as jnp
from jax import lax
from jax.experimental import pallas as pl
from jax.experimental.pallas import tpu as pltpu
from jax.sharding import PartitionSpec as P

HD = 64
BLK = 64
NB = 64


def _attend_kernel(g0, nbr_ref, cnt_ref, gain_ref, q_ref, bias_ref, kv_ref, o_ref):
    gi = g0 + pl.program_id(0)
    width = kv_ref.shape[-1]
    half_w = width // 2
    pairs = half_w // 128
    span = NB * BLK
    live_cols = cnt_ref[gi] * BLK
    col = lax.broadcasted_iota(jnp.int32, (BLK, span), 1)
    live = col < live_cols
    bias = bias_ref[0].astype(jnp.float32)
    q = q_ref[0]
    lane = lax.broadcasted_iota(jnp.int32, (BLK, 128), 1)
    scale = HD ** (-0.5)
    slots = [nbr_ref[gi, j] for j in range(NB)]
    outs = []
    for pair in range(pairs):
        k_lo = pair * 128
        v_lo = half_w + pair * 128
        kp = jnp.concatenate([kv_ref[b, :, k_lo:k_lo + 128] for b in slots], axis=0)
        vp = jnp.concatenate([kv_ref[b, :, v_lo:v_lo + 128] for b in slots], axis=0)
        qp = q[:, pair * 128:(pair + 1) * 128]
        res = None
        for half in range(2):
            h = pair * 2 + half
            in_head = (lane >= half * HD) & (lane < (half + 1) * HD)
            qm = jnp.where(in_head, qp, jnp.zeros_like(qp))
            s = lax.dot_general(
                qm, kp, (((1,), (1,)), ((), ())), preferred_element_type=jnp.float32
            )
            s = s * scale + gain_ref[h] * bias
            s = jnp.where(live, s, jnp.float32(-1e30))
            top = jnp.max(s, axis=1, keepdims=True)
            expo = jnp.exp(s - top)
            total = jnp.sum(expo, axis=1, keepdims=True)
            w = (expo * (1.0 / total)).astype(jnp.bfloat16)
            o = jnp.dot(w, vp, preferred_element_type=jnp.float32)
            res = o if res is None else jnp.where(lane < HD, res, o)
        outs.append(res.astype(jnp.bfloat16))
    o_ref[0] = jnp.concatenate(outs, axis=1)


def attend(nbr, cnt, gain, q_blocks, bias, kv_table, g0, steps):
    width_q = q_blocks.shape[-1]
    span = NB * BLK
    grid_spec = pltpu.PrefetchScalarGridSpec(
        num_scalar_prefetch=2,
        grid=(steps,),
        in_specs=[
            pl.BlockSpec(memory_space=pltpu.SMEM),
            pl.BlockSpec((1, BLK, width_q), lambda g, n, c: (g + g0, 0, 0)),
            pl.BlockSpec((1, BLK, span), lambda g, n, c: (g + g0, 0, 0)),
            pl.BlockSpec(kv_table.shape, lambda g, n, c: (0, 0, 0)),
        ],
        out_specs=pl.BlockSpec((1, BLK, width_q), lambda g, n, c: (g, 0, 0)),
    )
    return pl.pallas_call(
        functools.partial(_attend_kernel, g0),
        grid_spec=grid_spec,
        out_shape=jax.ShapeDtypeStruct((steps, BLK, width_q), jnp.bfloat16),
        compiler_params=pltpu.CompilerParams(
            dimension_semantics=("arbitrary",), vmem_limit_bytes=48 * 1024 * 1024
        ),
    )(nbr, cnt, gain, q_blocks, bias, kv_table)


def plan_requests(neighbours, per_owner, owners):
    owner = neighbours // per_owner
    local = neighbours % per_owner
    flat = neighbours.reshape(-1)
    ids = jnp.arange(owners * per_owner, dtype=jnp.int32)
    present = jnp.any(flat[:, None] == ids[None, :], axis=0).reshape(owners, per_owner)
    lidx = jnp.arange(per_owner, dtype=jnp.int32)[None, :]
    first = jnp.min(jnp.where(present, lidx, per_owner), axis=1)
    first = jnp.where(first == per_owner, 0, first)
    second = jnp.max(jnp.where(present, lidx, -1), axis=1)
    second = jnp.where(second < 0, first, second)
    req = jnp.stack([first, second], axis=1).astype(jnp.int32)
    pos = owner * 2 + (local != first[owner]).astype(jnp.int32)
    return req, pos.astype(jnp.int32)


def body(features, w_qkv, w_out, bias_gain, edge_bias, neighbours, counts):
    rows = features.shape[0]
    width_heads = w_qkv.shape[2]
    blocks_dev = rows // BLK
    head_devs = lax.axis_size("head")
    row_devs = lax.axis_size("row")
    me = lax.axis_index("head")
    req, pos = plan_requests(neighbours, blocks_dev, row_devs)
    wanted = lax.all_to_all(req, "row", 0, 0, tiled=True).reshape(-1)
    queries = jnp.dot(features, w_qkv[0], preferred_element_type=jnp.float32).astype(jnp.bfloat16)
    keys = jnp.dot(features, w_qkv[1], preferred_element_type=jnp.float32).astype(jnp.bfloat16)
    values = jnp.dot(features, w_qkv[2], preferred_element_type=jnp.float32).astype(jnp.bfloat16)
    kv = jnp.concatenate([keys, values], axis=1).reshape(blocks_dev, BLK, 2 * width_heads)
    outgoing = jnp.take(kv, wanted, axis=0, mode="clip")
    kv_table = lax.all_to_all(outgoing, "row", 0, 0, tiled=True)
    w_parts = []
    for s in range(1, head_devs):
        target = (me + s) % head_devs
        piece = lax.dynamic_slice_in_dim(w_out, target * width_heads, width_heads, axis=1)
        perm = [(i, (i + s) % head_devs) for i in range(head_devs)]
        w_parts.append(lax.ppermute(piece, "head", perm))
    w_own = lax.dynamic_slice_in_dim(w_out, me * width_heads, width_heads, axis=1)
    q_blocks = queries.reshape(blocks_dev, BLK, width_heads)
    halves = 2
    steps = blocks_dev // halves
    results = []
    for part in range(halves):
        att = attend(pos, counts, bias_gain, q_blocks, edge_bias, kv_table, part * steps, steps)
        att = att.reshape(steps * BLK, width_heads)
        total = jnp.dot(att, w_own, preferred_element_type=jnp.float32)
        for s in range(1, head_devs):
            perm = [(i, (i + s) % head_devs) for i in range(head_devs)]
            att_s = lax.ppermute(att, "head", perm)
            total = total + jnp.dot(att_s, w_parts[s - 1], preferred_element_type=jnp.float32)
        results.append(total.astype(jnp.bfloat16))
    return jnp.concatenate(results, axis=0)


def solution(mesh):
    in_specs = (
        P("row", None),
        P(None, None, "head"),
        P("head", None),
        P("head"),
        P("row", None, None),
        P("row", None),
        P("row"),
    )
    out_specs = P("row", "head")
    return jax.shard_map(body, mesh=mesh, in_specs=in_specs, out_specs=out_specs, check_vma=False)
```

```python
import functools

import jax
import jax.numpy as jnp
from jax import lax
from jax.experimental import pallas as pl
from jax.experimental.pallas import tpu as pltpu
from jax.sharding import PartitionSpec as P

HD = 64
BLK = 64
NB = 64


def _attend_kernel(p0, nbr_ref, cnt_ref, gain_ref, q_ref, bias_ref, kv_ref, o_ref):
    g = pl.program_id(0)
    width = kv_ref.shape[-1]
    half_w = width // 2
    pairs = half_w // 128
    span = NB * BLK
    live_cols = cnt_ref[g] * BLK
    col = lax.broadcasted_iota(jnp.int32, (BLK, span), 1)
    bias = jnp.where(col < live_cols, bias_ref[0].astype(jnp.float32), -jnp.inf)
    q = q_ref[0]
    lane = lax.broadcasted_iota(jnp.int32, (BLK, 128), 1)
    scale = HD ** (-0.5)
    slots = [nbr_ref[g, j] for j in range(NB)]
    outs = []
    for pair in range(pairs):
        k_lo = pair * 128
        v_lo = half_w + pair * 128
        kp = jnp.concatenate([kv_ref[b, :, k_lo:k_lo + 128] for b in slots], axis=0)
        vp = jnp.concatenate([kv_ref[b, :, v_lo:v_lo + 128] for b in slots], axis=0)
        qp = (q[:, pair * 128:(pair + 1) * 128].astype(jnp.float32) * scale).astype(jnp.bfloat16)
        res = None
        for half in range(2):
            h = (p0 + pair) * 2 + half
            in_head = (lane >= half * HD) & (lane < (half + 1) * HD)
            qm = jnp.where(in_head, qp, jnp.zeros_like(qp))
            s = lax.dot_general(
                qm, kp, (((1,), (1,)), ((), ())), preferred_element_type=jnp.float32
            )
            s = s + gain_ref[h] * bias
            top = jnp.max(s, axis=1, keepdims=True)
            expo = jnp.exp(s - top)
            total = jnp.sum(expo, axis=1, keepdims=True)
            w = (expo * (1.0 / total)).astype(jnp.bfloat16)
            o = jnp.dot(w, vp, preferred_element_type=jnp.float32)
            res = o if res is None else jnp.where(lane < HD, res, o)
        outs.append(res.astype(jnp.bfloat16))
    o_ref[0] = outs[0] if len(outs) == 1 else jnp.concatenate(outs, axis=1)


def attend(nbr, cnt, gain, q_blocks, bias, kv_table, p0, width_q):
    steps = q_blocks.shape[0]
    span = NB * BLK
    grid_spec = pltpu.PrefetchScalarGridSpec(
        num_scalar_prefetch=2,
        grid=(steps,),
        in_specs=[
            pl.BlockSpec(memory_space=pltpu.SMEM),
            pl.BlockSpec((1, BLK, width_q), lambda g, n, c: (g, 0, p0)),
            pl.BlockSpec((1, BLK, span), lambda g, n, c: (g, 0, 0)),
            pl.BlockSpec(kv_table.shape, lambda g, n, c: (0, 0, 0)),
        ],
        out_specs=pl.BlockSpec((1, BLK, width_q), lambda g, n, c: (g, 0, 0)),
    )
    return pl.pallas_call(
        functools.partial(_attend_kernel, p0),
        grid_spec=grid_spec,
        out_shape=jax.ShapeDtypeStruct((steps, BLK, width_q), jnp.bfloat16),
        compiler_params=pltpu.CompilerParams(
            dimension_semantics=("arbitrary",), vmem_limit_bytes=48 * 1024 * 1024
        ),
    )(nbr, cnt, gain, q_blocks, bias, kv_table)


def plan_requests(neighbours, per_owner, owners):
    owner = neighbours // per_owner
    local = neighbours % per_owner
    flat = neighbours.reshape(-1)
    ids = jnp.arange(owners * per_owner, dtype=jnp.int32)
    present = jnp.any(flat[:, None] == ids[None, :], axis=0).reshape(owners, per_owner)
    lidx = jnp.arange(per_owner, dtype=jnp.int32)[None, :]
    first = jnp.min(jnp.where(present, lidx, per_owner), axis=1)
    first = jnp.where(first == per_owner, 0, first)
    second = jnp.max(jnp.where(present, lidx, -1), axis=1)
    second = jnp.where(second < 0, first, second)
    req = jnp.stack([first, second], axis=1).astype(jnp.int32)
    pos = owner * 2 + (local != first[owner]).astype(jnp.int32)
    return req, pos.astype(jnp.int32)


def body(features, w_qkv, w_out, bias_gain, edge_bias, neighbours, counts):
    rows = features.shape[0]
    width_heads = w_qkv.shape[2]
    blocks_dev = rows // BLK
    head_devs = lax.axis_size("head")
    row_devs = lax.axis_size("row")
    me = lax.axis_index("head")
    chunk = 128
    chunks = width_heads // chunk
    req, pos = plan_requests(neighbours, blocks_dev, row_devs)
    wanted = lax.all_to_all(req, "row", 0, 0, tiled=True).reshape(-1)
    queries = jnp.dot(features, w_qkv[0], preferred_element_type=jnp.float32).astype(jnp.bfloat16)
    keys = jnp.dot(features, w_qkv[1], preferred_element_type=jnp.float32).astype(jnp.bfloat16)
    values = jnp.dot(features, w_qkv[2], preferred_element_type=jnp.float32).astype(jnp.bfloat16)
    w_parts = []
    for s in range(1, head_devs):
        target = (me + s) % head_devs
        piece = lax.dynamic_slice_in_dim(w_out, target * width_heads, width_heads, axis=1)
        perm = [(i, (i + s) % head_devs) for i in range(head_devs)]
        w_parts.append(lax.ppermute(piece, "head", perm))
    w_own = lax.dynamic_slice_in_dim(w_out, me * width_heads, width_heads, axis=1)
    q_blocks = queries.reshape(blocks_dev, BLK, width_heads)
    outgoing = []
    for c in range(chunks):
        cols = slice(c * chunk, (c + 1) * chunk)
        kv = jnp.concatenate([keys[:, cols], values[:, cols]], axis=1)
        kv = kv.reshape(blocks_dev, BLK, 2 * chunk)
        outgoing.append(jnp.take(kv, wanted, axis=0, mode="clip"))
    total = None
    table = None
    for c in range(chunks):
        cols = slice(c * chunk, (c + 1) * chunk)
        send = outgoing[c]
        if table is not None:
            table, send = lax.optimization_barrier((table, send))
        table = lax.all_to_all(send, "row", 0, 0, tiled=True)
        att = attend(pos, counts, bias_gain, q_blocks, edge_bias, table, c, chunk)
        att = att.reshape(rows, chunk)
        part = jnp.dot(att, w_own[cols], preferred_element_type=jnp.float32)
        total = part if total is None else total + part
        for s in range(1, head_devs):
            perm = [(i, (i + s) % head_devs) for i in range(head_devs)]
            att_s = lax.ppermute(att, "head", perm)
            total = total + jnp.dot(att_s, w_parts[s - 1][cols], preferred_element_type=jnp.float32)
    return total.astype(jnp.bfloat16)


def solution(mesh):
    in_specs = (
        P("row", None),
        P(None, None, "head"),
        P("head", None),
        P("head"),
        P("row", None, None),
        P("row", None),
        P("row"),
    )
    out_specs = P("row", "head")
    return jax.shard_map(body, mesh=mesh, in_specs=in_specs, out_specs=out_specs, check_vma=False)
```

```python
import functools

import jax
import jax.numpy as jnp
from jax import lax
from jax.experimental import pallas as pl
from jax.experimental.pallas import tpu as pltpu
from jax.sharding import PartitionSpec as P

HD = 64
BLK = 64
NB = 64


def _attend_kernel(p0, nbr_ref, cnt_ref, gain_ref, q_ref, bias_ref, kv_ref, o_ref):
    g = pl.program_id(0)
    width = kv_ref.shape[-1]
    half_w = width // 2
    pairs = half_w // 128
    span = NB * BLK
    live_cols = cnt_ref[g] * BLK
    col = lax.broadcasted_iota(jnp.int32, (BLK, span), 1)
    bias = jnp.where(col < live_cols, bias_ref[0].astype(jnp.float32), -jnp.inf)
    q = q_ref[0]
    lane = lax.broadcasted_iota(jnp.int32, (BLK, 128), 1)
    scale = HD ** (-0.5)
    slots = [nbr_ref[g, j] for j in range(NB)]
    outs = []
    for pair in range(pairs):
        k_lo = pair * 128
        v_lo = half_w + pair * 128
        kp = jnp.concatenate([kv_ref[b, :, k_lo:k_lo + 128] for b in slots], axis=0)
        vp = jnp.concatenate([kv_ref[b, :, v_lo:v_lo + 128] for b in slots], axis=0)
        qp = (q[:, pair * 128:(pair + 1) * 128].astype(jnp.float32) * scale).astype(jnp.bfloat16)
        res = None
        for half in range(2):
            h = (p0 + pair) * 2 + half
            in_head = (lane >= half * HD) & (lane < (half + 1) * HD)
            qm = jnp.where(in_head, qp, jnp.zeros_like(qp))
            s = lax.dot_general(
                qm, kp, (((1,), (1,)), ((), ())), preferred_element_type=jnp.float32
            )
            s = s + gain_ref[h] * bias
            top = jnp.max(s, axis=1, keepdims=True)
            expo = jnp.exp(s - top)
            total = jnp.sum(expo, axis=1, keepdims=True)
            w = (expo * (1.0 / total)).astype(jnp.bfloat16)
            o = jnp.dot(w, vp, preferred_element_type=jnp.float32)
            res = o if res is None else jnp.where(lane < HD, res, o)
        outs.append(res.astype(jnp.bfloat16))
    o_ref[0] = outs[0] if len(outs) == 1 else jnp.concatenate(outs, axis=1)


def attend(nbr, cnt, gain, q_blocks, bias, kv_table, p0, width_q):
    steps = q_blocks.shape[0]
    span = NB * BLK
    grid_spec = pltpu.PrefetchScalarGridSpec(
        num_scalar_prefetch=2,
        grid=(steps,),
        in_specs=[
            pl.BlockSpec(memory_space=pltpu.SMEM),
            pl.BlockSpec((1, BLK, width_q), lambda g, n, c: (g, 0, p0)),
            pl.BlockSpec((1, BLK, span), lambda g, n, c: (g, 0, 0)),
            pl.BlockSpec(kv_table.shape, lambda g, n, c: (0, 0, 0)),
        ],
        out_specs=pl.BlockSpec((1, BLK, width_q), lambda g, n, c: (g, 0, 0)),
    )
    return pl.pallas_call(
        functools.partial(_attend_kernel, p0),
        grid_spec=grid_spec,
        out_shape=jax.ShapeDtypeStruct((steps, BLK, width_q), jnp.bfloat16),
        compiler_params=pltpu.CompilerParams(
            dimension_semantics=("arbitrary",), vmem_limit_bytes=48 * 1024 * 1024
        ),
    )(nbr, cnt, gain, q_blocks, bias, kv_table)


def plan_requests(neighbours, per_owner, owners):
    owner = neighbours // per_owner
    local = neighbours % per_owner
    flat = neighbours.reshape(-1)
    ids = jnp.arange(owners * per_owner, dtype=jnp.int32)
    present = jnp.any(flat[:, None] == ids[None, :], axis=0).reshape(owners, per_owner)
    lidx = jnp.arange(per_owner, dtype=jnp.int32)[None, :]
    first = jnp.min(jnp.where(present, lidx, per_owner), axis=1)
    first = jnp.where(first == per_owner, 0, first)
    second = jnp.max(jnp.where(present, lidx, -1), axis=1)
    second = jnp.where(second < 0, first, second)
    req = jnp.stack([first, second], axis=1).astype(jnp.int32)
    pos = owner * 2 + (local != first[owner]).astype(jnp.int32)
    return req, pos.astype(jnp.int32)


def body(features, w_qkv, w_out, bias_gain, edge_bias, neighbours, counts):
    rows = features.shape[0]
    width_heads = w_qkv.shape[2]
    blocks_dev = rows // BLK
    head_devs = lax.axis_size("head")
    row_devs = lax.axis_size("row")
    me = lax.axis_index("head")
    chunk = 128
    chunks = width_heads // chunk
    req, pos = plan_requests(neighbours, blocks_dev, row_devs)
    wanted = lax.all_to_all(req, "row", 0, 0, tiled=True).reshape(-1)
    queries = jnp.dot(features, w_qkv[0], preferred_element_type=jnp.float32).astype(jnp.bfloat16)
    keys = jnp.dot(features, w_qkv[1], preferred_element_type=jnp.float32).astype(jnp.bfloat16)
    values = jnp.dot(features, w_qkv[2], preferred_element_type=jnp.float32).astype(jnp.bfloat16)
    w_full = lax.all_gather(w_out, "head", axis=0, tiled=True)
    w_cols = lax.dynamic_slice_in_dim(w_full, me * width_heads, width_heads, axis=1)
    q_blocks = queries.reshape(blocks_dev, BLK, width_heads)
    outgoing = []
    for c in range(chunks):
        cols = slice(c * chunk, (c + 1) * chunk)
        kv = jnp.concatenate([keys[:, cols], values[:, cols]], axis=1)
        kv = kv.reshape(blocks_dev, BLK, 2 * chunk)
        outgoing.append(jnp.take(kv, wanted, axis=0, mode="clip"))
    pieces = []
    w_pieces = []
    table = None
    for c in range(chunks):
        send = outgoing[c]
        if table is not None:
            table, send = lax.optimization_barrier((table, send))
        table = lax.all_to_all(send, "row", 0, 0, tiled=True)
        att = attend(pos, counts, bias_gain, q_blocks, edge_bias, table, c, chunk)
        att = att.reshape(rows, chunk)
        for s in range(head_devs):
            if s == 0:
                pieces.append(att)
            else:
                perm = [(i, (i + s) % head_devs) for i in range(head_devs)]
                pieces.append(lax.ppermute(att, "head", perm))
            src = (me - s) % head_devs
            w_pieces.append(
                lax.dynamic_slice_in_dim(w_cols, src * width_heads + c * chunk, chunk, axis=0)
            )
    att_all = jnp.concatenate(pieces, axis=1)
    w_all = jnp.concatenate(w_pieces, axis=0)
    return jnp.dot(att_all, w_all, preferred_element_type=jnp.float32).astype(jnp.bfloat16)


def solution(mesh):
    in_specs = (
        P("row", None),
        P(None, None, "head"),
        P("head", None),
        P("head"),
        P("row", None, None),
        P("row", None),
        P("row"),
    )
    out_specs = P("row", "head")
    return jax.shard_map(body, mesh=mesh, in_specs=in_specs, out_specs=out_specs, check_vma=False)
```

```python
import functools

import jax
import jax.numpy as jnp
from jax import lax
from jax.experimental import pallas as pl
from jax.experimental.pallas import tpu as pltpu
from jax.sharding import PartitionSpec as P

HD = 64
BLK = 64
NB = 64


def _attend_kernel(p0, nbr_ref, cnt_ref, gain_ref, q_ref, bias_ref, kv_ref, o_ref):
    g = pl.program_id(0)
    width = kv_ref.shape[-1]
    half_w = width // 2
    pairs = half_w // 128
    span = NB * BLK
    live_cols = cnt_ref[g] * BLK
    col = lax.broadcasted_iota(jnp.int32, (BLK, span), 1)
    bias = jnp.where(col < live_cols, bias_ref[0].astype(jnp.float32), -jnp.inf)
    q = q_ref[0]
    lane = lax.broadcasted_iota(jnp.int32, (BLK, 128), 1)
    scale = HD ** (-0.5)
    slots = [nbr_ref[g, j] for j in range(NB)]
    outs = []
    for pair in range(pairs):
        k_lo = pair * 128
        v_lo = half_w + pair * 128
        kp = jnp.concatenate([kv_ref[b, :, k_lo:k_lo + 128] for b in slots], axis=0)
        vp = jnp.concatenate([kv_ref[b, :, v_lo:v_lo + 128] for b in slots], axis=0)
        qp = (q[:, pair * 128:(pair + 1) * 128].astype(jnp.float32) * scale).astype(jnp.bfloat16)
        zeros = jnp.zeros_like(qp)
        q2 = jnp.concatenate(
            [jnp.where(lane < HD, qp, zeros), jnp.where(lane >= HD, qp, zeros)], axis=0
        )
        s2 = lax.dot_general(
            q2, kp, (((1,), (1,)), ((), ())), preferred_element_type=jnp.float32
        )
        ws = []
        for half in range(2):
            h = (p0 + pair) * 2 + half
            s = s2[half * BLK:(half + 1) * BLK] + gain_ref[h] * bias
            top = jnp.max(s, axis=1, keepdims=True)
            expo = jnp.exp(s - top)
            total = jnp.sum(expo, axis=1, keepdims=True)
            ws.append((expo * (1.0 / total)).astype(jnp.bfloat16))
        o2 = jnp.dot(jnp.concatenate(ws, axis=0), vp, preferred_element_type=jnp.float32)
        res = jnp.where(lane < HD, o2[:BLK], o2[BLK:])
        outs.append(res.astype(jnp.bfloat16))
    o_ref[0] = outs[0] if len(outs) == 1 else jnp.concatenate(outs, axis=1)


def attend(nbr, cnt, gain, q_blocks, bias, kv_table, p0, width_q):
    steps = q_blocks.shape[0]
    span = NB * BLK
    grid_spec = pltpu.PrefetchScalarGridSpec(
        num_scalar_prefetch=2,
        grid=(steps,),
        in_specs=[
            pl.BlockSpec(memory_space=pltpu.SMEM),
            pl.BlockSpec((1, BLK, width_q), lambda g, n, c: (g, 0, p0)),
            pl.BlockSpec((1, BLK, span), lambda g, n, c: (g, 0, 0)),
            pl.BlockSpec(kv_table.shape, lambda g, n, c: (0, 0, 0)),
        ],
        out_specs=pl.BlockSpec((1, BLK, width_q), lambda g, n, c: (g, 0, 0)),
    )
    return pl.pallas_call(
        functools.partial(_attend_kernel, p0),
        grid_spec=grid_spec,
        out_shape=jax.ShapeDtypeStruct((steps, BLK, width_q), jnp.bfloat16),
        compiler_params=pltpu.CompilerParams(
            dimension_semantics=("arbitrary",), vmem_limit_bytes=48 * 1024 * 1024
        ),
    )(nbr, cnt, gain, q_blocks, bias, kv_table)


def plan_requests(neighbours, per_owner, owners):
    owner = neighbours // per_owner
    local = neighbours % per_owner
    flat = neighbours.reshape(-1)
    ids = jnp.arange(owners * per_owner, dtype=jnp.int32)
    present = jnp.any(flat[:, None] == ids[None, :], axis=0).reshape(owners, per_owner)
    lidx = jnp.arange(per_owner, dtype=jnp.int32)[None, :]
    first = jnp.min(jnp.where(present, lidx, per_owner), axis=1)
    first = jnp.where(first == per_owner, 0, first)
    second = jnp.max(jnp.where(present, lidx, -1), axis=1)
    second = jnp.where(second < 0, first, second)
    req = jnp.stack([first, second], axis=1).astype(jnp.int32)
    pos = owner * 2 + (local != first[owner]).astype(jnp.int32)
    return req, pos.astype(jnp.int32)


def body(features, w_qkv, w_out, bias_gain, edge_bias, neighbours, counts):
    rows = features.shape[0]
    width_heads = w_qkv.shape[2]
    blocks_dev = rows // BLK
    head_devs = lax.axis_size("head")
    row_devs = lax.axis_size("row")
    me = lax.axis_index("head")
    chunk = 128
    chunks = width_heads // chunk
    req, pos = plan_requests(neighbours, blocks_dev, row_devs)
    wanted = lax.all_to_all(req, "row", 0, 0, tiled=True).reshape(-1)
    queries = jnp.dot(features, w_qkv[0], preferred_element_type=jnp.float32).astype(jnp.bfloat16)
    keys = jnp.dot(features, w_qkv[1], preferred_element_type=jnp.float32).astype(jnp.bfloat16)
    values = jnp.dot(features, w_qkv[2], preferred_element_type=jnp.float32).astype(jnp.bfloat16)
    w_parts = []
    for s in range(1, head_devs):
        target = (me + s) % head_devs
        piece = lax.dynamic_slice_in_dim(w_out, target * width_heads, width_heads, axis=1)
        perm = [(i, (i + s) % head_devs) for i in range(head_devs)]
        w_parts.append(lax.ppermute(piece, "head", perm))
    w_own = lax.dynamic_slice_in_dim(w_out, me * width_heads, width_heads, axis=1)
    q_blocks = queries.reshape(blocks_dev, BLK, width_heads)
    outgoing = []
    for c in range(chunks):
        cols = slice(c * chunk, (c + 1) * chunk)
        kv = jnp.concatenate([keys[:, cols], values[:, cols]], axis=1)
        kv = kv.reshape(blocks_dev, BLK, 2 * chunk)
        outgoing.append(jnp.take(kv, wanted, axis=0, mode="clip"))
    total = None
    table = None
    for c in range(chunks):
        cols = slice(c * chunk, (c + 1) * chunk)
        send = outgoing[c]
        if table is not None:
            table, send = lax.optimization_barrier((table, send))
        table = lax.all_to_all(send, "row", 0, 0, tiled=True)
        att = attend(pos, counts, bias_gain, q_blocks, edge_bias, table, c, chunk)
        att = att.reshape(rows, chunk)
        part = jnp.dot(att, w_own[cols], preferred_element_type=jnp.float32)
        total = part if total is None else total + part
        for s in range(1, head_devs):
            perm = [(i, (i + s) % head_devs) for i in range(head_devs)]
            att_s = lax.ppermute(att, "head", perm)
            total = total + jnp.dot(att_s, w_parts[s - 1][cols], preferred_element_type=jnp.float32)
    return total.astype(jnp.bfloat16)


def solution(mesh):
    in_specs = (
        P("row", None),
        P(None, None, "head"),
        P("head", None),
        P("head"),
        P("row", None, None),
        P("row", None),
        P("row"),
    )
    out_specs = P("row", "head")
    return jax.shard_map(body, mesh=mesh, in_specs=in_specs, out_specs=out_specs, check_vma=False)
```

```python
import functools

import jax
import jax.numpy as jnp
from jax import lax
from jax.experimental import pallas as pl
from jax.experimental.pallas import tpu as pltpu
from jax.sharding import PartitionSpec as P

HD = 64
BLK = 64
NB = 64


def _attend_kernel(p0, nbr_ref, cnt_ref, gain_ref, q_ref, bias_ref, kv_ref, o_ref):
    g = pl.program_id(0)
    width = kv_ref.shape[-1]
    half_w = width // 2
    pairs = half_w // 128
    span = NB * BLK
    live_cols = cnt_ref[g] * BLK
    col = lax.broadcasted_iota(jnp.int32, (BLK, span), 1)
    bias = jnp.where(col < live_cols, bias_ref[0].astype(jnp.float32), -jnp.inf)
    q = q_ref[0]
    lane = lax.broadcasted_iota(jnp.int32, (BLK, 128), 1)
    scale = HD ** (-0.5)
    slots = [nbr_ref[g, j] for j in range(NB)]
    outs = []
    for pair in range(pairs):
        k_lo = pair * 128
        v_lo = half_w + pair * 128
        kp = jnp.concatenate([kv_ref[b, :, k_lo:k_lo + 128] for b in slots], axis=0)
        vp = jnp.concatenate([kv_ref[b, :, v_lo:v_lo + 128] for b in slots], axis=0)
        qp = (q[:, pair * 128:(pair + 1) * 128].astype(jnp.float32) * scale).astype(jnp.bfloat16)
        zeros = jnp.zeros_like(qp)
        q2 = jnp.concatenate(
            [jnp.where(lane < HD, qp, zeros), jnp.where(lane >= HD, qp, zeros)], axis=0
        )
        s2 = lax.dot_general(
            q2, kp, (((1,), (1,)), ((), ())), preferred_element_type=jnp.float32
        )
        ws = []
        for half in range(2):
            h = (p0 + pair) * 2 + half
            s = s2[half * BLK:(half + 1) * BLK] + gain_ref[h] * bias
            top = jnp.max(s, axis=1, keepdims=True)
            expo = jnp.exp(s - top)
            total = jnp.sum(expo, axis=1, keepdims=True)
            ws.append((expo * (1.0 / total)).astype(jnp.bfloat16))
        o2 = jnp.dot(jnp.concatenate(ws, axis=0), vp, preferred_element_type=jnp.float32)
        res = jnp.where(lane < HD, o2[:BLK], o2[BLK:])
        outs.append(res.astype(jnp.bfloat16))
    o_ref[0] = outs[0] if len(outs) == 1 else jnp.concatenate(outs, axis=1)


def attend(nbr, cnt, gain, q_blocks, bias, kv_table, p0, width_q):
    steps = q_blocks.shape[0]
    span = NB * BLK
    grid_spec = pltpu.PrefetchScalarGridSpec(
        num_scalar_prefetch=2,
        grid=(steps,),
        in_specs=[
            pl.BlockSpec(memory_space=pltpu.SMEM),
            pl.BlockSpec((1, BLK, width_q), lambda g, n, c: (g, 0, p0)),
            pl.BlockSpec((1, BLK, span), lambda g, n, c: (g, 0, 0)),
            pl.BlockSpec(kv_table.shape, lambda g, n, c: (0, 0, 0)),
        ],
        out_specs=pl.BlockSpec((1, BLK, width_q), lambda g, n, c: (g, 0, 0)),
    )
    return pl.pallas_call(
        functools.partial(_attend_kernel, p0),
        grid_spec=grid_spec,
        out_shape=jax.ShapeDtypeStruct((steps, BLK, width_q), jnp.bfloat16),
        compiler_params=pltpu.CompilerParams(
            dimension_semantics=("arbitrary",), vmem_limit_bytes=48 * 1024 * 1024
        ),
    )(nbr, cnt, gain, q_blocks, bias, kv_table)


def plan_requests(neighbours, per_owner, owners):
    owner = neighbours // per_owner
    local = neighbours % per_owner
    flat = neighbours.reshape(-1)
    ids = jnp.arange(owners * per_owner, dtype=jnp.int32)
    present = jnp.any(flat[:, None] == ids[None, :], axis=0).reshape(owners, per_owner)
    lidx = jnp.arange(per_owner, dtype=jnp.int32)[None, :]
    first = jnp.min(jnp.where(present, lidx, per_owner), axis=1)
    first = jnp.where(first == per_owner, 0, first)
    second = jnp.max(jnp.where(present, lidx, -1), axis=1)
    second = jnp.where(second < 0, first, second)
    req = jnp.stack([first, second], axis=1).astype(jnp.int32)
    hit = owner.reshape(-1)[:, None] == jnp.arange(owners, dtype=jnp.int32)[None, :]
    first_of = jnp.sum(jnp.where(hit, first[None, :], 0), axis=1).reshape(owner.shape)
    pos = owner * 2 + (local != first_of).astype(jnp.int32)
    return req, pos.astype(jnp.int32)


def body(features, w_qkv, w_out, bias_gain, edge_bias, neighbours, counts):
    rows = features.shape[0]
    width_heads = w_qkv.shape[2]
    blocks_dev = rows // BLK
    head_devs = lax.axis_size("head")
    row_devs = lax.axis_size("row")
    me = lax.axis_index("head")
    chunk = 128
    chunks = width_heads // chunk
    req, pos = plan_requests(neighbours, blocks_dev, row_devs)
    wanted = lax.all_to_all(req, "row", 0, 0, tiled=True).reshape(-1)
    queries = jnp.dot(features, w_qkv[0], preferred_element_type=jnp.float32).astype(jnp.bfloat16)
    keys = jnp.dot(features, w_qkv[1], preferred_element_type=jnp.float32).astype(jnp.bfloat16)
    values = jnp.dot(features, w_qkv[2], preferred_element_type=jnp.float32).astype(jnp.bfloat16)
    w_parts = []
    for s in range(1, head_devs):
        target = (me + s) % head_devs
        piece = lax.dynamic_slice_in_dim(w_out, target * width_heads, width_heads, axis=1)
        perm = [(i, (i + s) % head_devs) for i in range(head_devs)]
        w_parts.append(lax.ppermute(piece, "head", perm))
    w_own = lax.dynamic_slice_in_dim(w_out, me * width_heads, width_heads, axis=1)
    q_blocks = queries.reshape(blocks_dev, BLK, width_heads)
    outgoing = []
    for c in range(chunks):
        cols = slice(c * chunk, (c + 1) * chunk)
        kv = jnp.concatenate([keys[:, cols], values[:, cols]], axis=1)
        kv = kv.reshape(blocks_dev, BLK, 2 * chunk)
        outgoing.append(jnp.take(kv, wanted, axis=0, mode="clip"))
    total = None
    table = None
    for c in range(chunks):
        cols = slice(c * chunk, (c + 1) * chunk)
        send = outgoing[c]
        if table is not None:
            table, send = lax.optimization_barrier((table, send))
        table = lax.all_to_all(send, "row", 0, 0, tiled=True)
        att = attend(pos, counts, bias_gain, q_blocks, edge_bias, table, c, chunk)
        att = att.reshape(rows, chunk)
        att_all = [att]
        w_all = [w_own[cols]]
        for s in range(1, head_devs):
            perm = [(i, (i + s) % head_devs) for i in range(head_devs)]
            att_all.append(lax.ppermute(att, "head", perm))
            w_all.append(w_parts[s - 1][cols])
        part = jnp.dot(
            jnp.concatenate(att_all, axis=1),
            jnp.concatenate(w_all, axis=0),
            preferred_element_type=jnp.float32,
        )
        total = part if total is None else total + part
    return total.astype(jnp.bfloat16)


def solution(mesh):
    in_specs = (
        P("row", None),
        P(None, None, "head"),
        P("head", None),
        P("head"),
        P("row", None, None),
        P("row", None),
        P("row"),
    )
    out_specs = P("row", "head")
    return jax.shard_map(body, mesh=mesh, in_specs=in_specs, out_specs=out_specs, check_vma=False)
```

```python
import functools

import jax
import jax.numpy as jnp
from jax import lax
from jax.experimental import pallas as pl
from jax.experimental.pallas import tpu as pltpu
from jax.sharding import PartitionSpec as P


HD = 64
BLK = 64
NB = 64


def _attend_kernel(p0, g0, nbr_ref, cnt_ref, gain_ref, q_ref, bias_ref, kv_ref, o_ref):
    g = g0 + pl.program_id(0)
    width = kv_ref.shape[-1]
    half_w = width // 2
    pairs = half_w // 128
    span = NB * BLK
    live_cols = cnt_ref[g] * BLK
    col = lax.broadcasted_iota(jnp.int32, (BLK, span), 1)
    bias = jnp.where(col < live_cols, bias_ref[0].astype(jnp.float32), -jnp.inf)
    q = q_ref[0]
    lane = lax.broadcasted_iota(jnp.int32, (BLK, 128), 1)
    scale = HD ** (-0.5)
    slots = [nbr_ref[g, j] for j in range(NB)]
    outs = []
    for pair in range(pairs):
        k_lo = pair * 128
        v_lo = half_w + pair * 128
        kp = jnp.concatenate([kv_ref[b, :, k_lo:k_lo + 128] for b in slots], axis=0)
        vp = jnp.concatenate([kv_ref[b, :, v_lo:v_lo + 128] for b in slots], axis=0)
        qp = (q[:, pair * 128:(pair + 1) * 128].astype(jnp.float32) * scale).astype(jnp.bfloat16)
        zeros = jnp.zeros_like(qp)
        q2 = jnp.concatenate(
            [jnp.where(lane < HD, qp, zeros), jnp.where(lane >= HD, qp, zeros)], axis=0
        )
        s2 = lax.dot_general(
            q2, kp, (((1,), (1,)), ((), ())), preferred_element_type=jnp.float32
        )
        ws = []
        sums = []
        for half in range(2):
            h = (p0 + pair) * 2 + half
            s = s2[half * BLK:(half + 1) * BLK] + gain_ref[h] * bias
            top = jnp.max(s, axis=1, keepdims=True)
            expo = jnp.exp(s - top)
            sums.append(jnp.sum(expo, axis=1, keepdims=True))
            ws.append(expo.astype(jnp.bfloat16))
        o2 = jnp.dot(jnp.concatenate(ws, axis=0), vp, preferred_element_type=jnp.float32)
        o2 = o2 * (1.0 / jnp.concatenate(sums, axis=0))
        res = jnp.where(lane < HD, o2[:BLK], o2[BLK:])
        outs.append(res.astype(jnp.bfloat16))
    o_ref[0] = outs[0] if len(outs) == 1 else jnp.concatenate(outs, axis=1)


def attend(nbr, cnt, gain, q_blocks, bias, kv_table, p0, width_q, g0, steps):
    span = NB * BLK
    grid_spec = pltpu.PrefetchScalarGridSpec(
        num_scalar_prefetch=2,
        grid=(steps,),
        in_specs=[
            pl.BlockSpec(memory_space=pltpu.SMEM),
            pl.BlockSpec((1, BLK, width_q), lambda g, n, c: (g + g0, 0, p0)),
            pl.BlockSpec((1, BLK, span), lambda g, n, c: (g + g0, 0, 0)),
            pl.BlockSpec(kv_table.shape, lambda g, n, c: (0, 0, 0)),
        ],
        out_specs=pl.BlockSpec((1, BLK, width_q), lambda g, n, c: (g, 0, 0)),
    )
    return pl.pallas_call(
        functools.partial(_attend_kernel, p0, g0),
        grid_spec=grid_spec,
        out_shape=jax.ShapeDtypeStruct((steps, BLK, width_q), jnp.bfloat16),
        compiler_params=pltpu.CompilerParams(
            dimension_semantics=("arbitrary",), vmem_limit_bytes=48 * 1024 * 1024
        ),
    )(nbr, cnt, gain, q_blocks, bias, kv_table)


def plan_requests(neighbours, per_owner, owners):
    owner = neighbours // per_owner
    local = neighbours % per_owner
    flat = neighbours.reshape(-1)
    ids = jnp.arange(owners * per_owner, dtype=jnp.int32)
    present = jnp.any(flat[:, None] == ids[None, :], axis=0).reshape(owners, per_owner)
    lidx = jnp.arange(per_owner, dtype=jnp.int32)[None, :]
    first = jnp.min(jnp.where(present, lidx, per_owner), axis=1)
    first = jnp.where(first == per_owner, 0, first)
    second = jnp.max(jnp.where(present, lidx, -1), axis=1)
    second = jnp.where(second < 0, first, second)
    req = jnp.stack([first, second], axis=1).astype(jnp.int32)
    hit = owner.reshape(-1)[:, None] == jnp.arange(owners, dtype=jnp.int32)[None, :]
    first_of = jnp.sum(jnp.where(hit, first[None, :], 0), axis=1).reshape(owner.shape)
    pos = owner * 2 + (local != first_of).astype(jnp.int32)
    return req, pos.astype(jnp.int32)


def _body(features, w_qkv, w_out, bias_gain, edge_bias, neighbours, counts):
    rows = features.shape[0]
    width_heads = w_qkv.shape[2]
    blocks_dev = rows // BLK
    head_devs = lax.axis_size("head")
    row_devs = lax.axis_size("row")
    me = lax.axis_index("head")
    chunk = 128
    chunks = width_heads // chunk
    req, pos = plan_requests(neighbours, blocks_dev, row_devs)
    wanted = lax.all_to_all(req, "row", 0, 0, tiled=True).reshape(-1)
    queries = jnp.dot(features, w_qkv[0], preferred_element_type=jnp.float32).astype(jnp.bfloat16)
    keys = jnp.dot(features, w_qkv[1], preferred_element_type=jnp.float32).astype(jnp.bfloat16)
    values = jnp.dot(features, w_qkv[2], preferred_element_type=jnp.float32).astype(jnp.bfloat16)
    w_parts = []
    for s in range(1, head_devs):
        target = (me + s) % head_devs
        piece = lax.dynamic_slice_in_dim(w_out, target * width_heads, width_heads, axis=1)
        perm = [(i, (i + s) % head_devs) for i in range(head_devs)]
        w_parts.append(lax.ppermute(piece, "head", perm))
    w_own = lax.dynamic_slice_in_dim(w_out, me * width_heads, width_heads, axis=1)
    q_blocks = queries.reshape(blocks_dev, BLK, width_heads)
    outgoing = []
    for c in range(chunks):
        cols = slice(c * chunk, (c + 1) * chunk)
        kv = jnp.concatenate([keys[:, cols], values[:, cols]], axis=1)
        kv = kv.reshape(blocks_dev, BLK, 2 * chunk)
        outgoing.append(jnp.take(kv, wanted, axis=0, mode="clip"))
    total = None
    table = None
    for c in range(chunks):
        cols = slice(c * chunk, (c + 1) * chunk)
        send = outgoing[c]
        if table is not None:
            table, send = lax.optimization_barrier((table, send))
        table = lax.all_to_all(send, "row", 0, 0, tiled=True)
        splits = 1 if c == 0 else 2
        steps = blocks_dev // splits
        for half in range(splits):
            rs = slice(half * steps * BLK, (half + 1) * steps * BLK)
            att = attend(
                pos, counts, bias_gain, q_blocks, edge_bias, table, c, chunk, half * steps, steps
            ).reshape(steps * BLK, chunk)
            att_all = [att]
            w_all = [w_own[cols]]
            for s in range(1, head_devs):
                perm = [(i, (i + s) % head_devs) for i in range(head_devs)]
                att_all.append(lax.ppermute(att, "head", perm))
                w_all.append(w_parts[s - 1][cols])
            part = jnp.dot(
                jnp.concatenate(att_all, axis=1),
                jnp.concatenate(w_all, axis=0),
                preferred_element_type=jnp.float32,
            )
            if total is None:
                total = part
            else:
                total = total.at[rs].add(part)
    return total.astype(jnp.bfloat16)


def solution(mesh):
    in_specs = (
        P("row", None),
        P(None, None, "head"),
        P("head", None),
        P("head"),
        P("row", None, None),
        P("row", None),
        P("row"),
    )
    out_specs = P("row", "head")
    return jax.shard_map(_body, mesh=mesh, in_specs=in_specs, out_specs=out_specs, check_vma=False)
```

```python
import functools

import jax
import jax.numpy as jnp
from jax import lax
from jax.experimental import pallas as pl
from jax.experimental.pallas import tpu as pltpu
from jax.sharding import PartitionSpec as P


HD = 64
BLK = 64
NB = 64


def _attend_kernel(p0, nbr_ref, cnt_ref, gain_ref, q_ref, bias_ref, kv_ref, o_ref):
    g = pl.program_id(0)
    width = kv_ref.shape[-1]
    half_w = width // 2
    pairs = half_w // 128
    span = NB * BLK
    live_cols = cnt_ref[g] * BLK
    col = lax.broadcasted_iota(jnp.int32, (BLK, span), 1)
    bias = jnp.where(col < live_cols, bias_ref[0].astype(jnp.float32), -jnp.inf)
    q = q_ref[0]
    lane = lax.broadcasted_iota(jnp.int32, (BLK, 128), 1)
    scale = HD ** (-0.5)
    slots = [nbr_ref[g, j] for j in range(NB)]
    outs = []
    for pair in range(pairs):
        k_lo = pair * 128
        v_lo = half_w + pair * 128
        kp = jnp.concatenate([kv_ref[b, :, k_lo:k_lo + 128] for b in slots], axis=0)
        vp = jnp.concatenate([kv_ref[b, :, v_lo:v_lo + 128] for b in slots], axis=0)
        qp = (q[:, pair * 128:(pair + 1) * 128].astype(jnp.float32) * scale).astype(jnp.bfloat16)
        zeros = jnp.zeros_like(qp)
        q2 = jnp.concatenate(
            [jnp.where(lane < HD, qp, zeros), jnp.where(lane >= HD, qp, zeros)], axis=0
        )
        s2 = lax.dot_general(
            q2, kp, (((1,), (1,)), ((), ())), preferred_element_type=jnp.float32
        )
        ws = []
        sums = []
        for half in range(2):
            h = (p0 + pair) * 2 + half
            s = s2[half * BLK:(half + 1) * BLK] + gain_ref[h] * bias
            top = jnp.max(s, axis=1, keepdims=True)
            expo = jnp.exp(s - top)
            sums.append(jnp.sum(expo, axis=1, keepdims=True))
            ws.append(expo.astype(jnp.bfloat16))
        o2 = jnp.dot(jnp.concatenate(ws, axis=0), vp, preferred_element_type=jnp.float32)
        o2 = o2 * (1.0 / jnp.concatenate(sums, axis=0))
        res = jnp.where(lane < HD, o2[:BLK], o2[BLK:])
        outs.append(res.astype(jnp.bfloat16))
    o_ref[0] = outs[0] if len(outs) == 1 else jnp.concatenate(outs, axis=1)


def attend(nbr, cnt, gain, q_blocks, bias, kv_table, p0, width_q):
    steps = q_blocks.shape[0]
    span = NB * BLK
    grid_spec = pltpu.PrefetchScalarGridSpec(
        num_scalar_prefetch=2,
        grid=(steps,),
        in_specs=[
            pl.BlockSpec(memory_space=pltpu.SMEM),
            pl.BlockSpec((1, BLK, width_q), lambda g, n, c: (g, 0, p0)),
            pl.BlockSpec((1, BLK, span), lambda g, n, c: (g, 0, 0)),
            pl.BlockSpec(kv_table.shape, lambda g, n, c: (0, 0, 0)),
        ],
        out_specs=pl.BlockSpec((1, BLK, width_q), lambda g, n, c: (g, 0, 0)),
    )
    return pl.pallas_call(
        functools.partial(_attend_kernel, p0),
        grid_spec=grid_spec,
        out_shape=jax.ShapeDtypeStruct((steps, BLK, width_q), jnp.bfloat16),
        compiler_params=pltpu.CompilerParams(
            dimension_semantics=("arbitrary",), vmem_limit_bytes=48 * 1024 * 1024
        ),
    )(nbr, cnt, gain, q_blocks, bias, kv_table)


def plan_requests(neighbours, per_owner, owners):
    owner = neighbours // per_owner
    local = neighbours % per_owner
    flat = neighbours.reshape(-1)
    ids = jnp.arange(owners * per_owner, dtype=jnp.int32)
    present = jnp.any(flat[:, None] == ids[None, :], axis=0).reshape(owners, per_owner)
    lidx = jnp.arange(per_owner, dtype=jnp.int32)[None, :]
    first = jnp.min(jnp.where(present, lidx, per_owner), axis=1)
    first = jnp.where(first == per_owner, 0, first)
    second = jnp.max(jnp.where(present, lidx, -1), axis=1)
    second = jnp.where(second < 0, first, second)
    req = jnp.stack([first, second], axis=1).astype(jnp.int32)
    hit = owner.reshape(-1)[:, None] == jnp.arange(owners, dtype=jnp.int32)[None, :]
    first_of = jnp.sum(jnp.where(hit, first[None, :], 0), axis=1).reshape(owner.shape)
    pos = owner * 2 + (local != first_of).astype(jnp.int32)
    return req, pos.astype(jnp.int32)


def _body(features, w_qkv, w_out, bias_gain, edge_bias, neighbours, counts):
    rows = features.shape[0]
    width_heads = w_qkv.shape[2]
    blocks_dev = rows // BLK
    head_devs = lax.axis_size("head")
    row_devs = lax.axis_size("row")
    me = lax.axis_index("head")
    chunk = 128
    chunks = width_heads // chunk
    req, pos = plan_requests(neighbours, blocks_dev, row_devs)
    wanted = lax.all_to_all(req, "row", 0, 0, tiled=True).reshape(-1)
    queries = jnp.dot(features, w_qkv[0], preferred_element_type=jnp.float32).astype(jnp.bfloat16)
    keys = jnp.dot(features, w_qkv[1], preferred_element_type=jnp.float32).astype(jnp.bfloat16)
    values = jnp.dot(features, w_qkv[2], preferred_element_type=jnp.float32).astype(jnp.bfloat16)
    w_parts = []
    for s in range(1, head_devs):
        target = (me + s) % head_devs
        piece = lax.dynamic_slice_in_dim(w_out, target * width_heads, width_heads, axis=1)
        perm = [(i, (i + s) % head_devs) for i in range(head_devs)]
        w_parts.append(lax.ppermute(piece, "head", perm))
    w_own = lax.dynamic_slice_in_dim(w_out, me * width_heads, width_heads, axis=1)
    q_blocks = queries.reshape(blocks_dev, BLK, width_heads)
    outgoing = []
    for c in range(chunks):
        cols = slice(c * chunk, (c + 1) * chunk)
        kv = jnp.concatenate([keys[:, cols], values[:, cols]], axis=1)
        kv = kv.reshape(blocks_dev, BLK, 2 * chunk)
        outgoing.append(jnp.take(kv, wanted, axis=0, mode="clip"))
    total = None
    table = None
    for c in range(chunks):
        cols = slice(c * chunk, (c + 1) * chunk)
        send = outgoing[c]
        if table is not None:
            table, send = lax.optimization_barrier((table, send))
        table = lax.all_to_all(send, "row", 0, 0, tiled=True)
        att = attend(pos, counts, bias_gain, q_blocks, edge_bias, table, c, chunk)
        att = att.reshape(rows, chunk)
        att_all = [att]
        w_all = [w_own[cols]]
        for s in range(1, head_devs):
            perm = [(i, (i + s) % head_devs) for i in range(head_devs)]
            att_all.append(lax.ppermute(att, "head", perm))
            w_all.append(w_parts[s - 1][cols])
        part = jnp.dot(
            jnp.concatenate(att_all, axis=1),
            jnp.concatenate(w_all, axis=0),
            preferred_element_type=jnp.float32,
        )
        total = part if total is None else total + part
    return total.astype(jnp.bfloat16)


def solution(mesh):
    in_specs = (
        P("row", None),
        P(None, None, "head"),
        P("head", None),
        P("head"),
        P("row", None, None),
        P("row", None),
        P("row"),
    )
    out_specs = P("row", "head")
    return jax.shard_map(_body, mesh=mesh, in_specs=in_specs, out_specs=out_specs, check_vma=False)
```

```python
import functools

import jax
import jax.numpy as jnp
from jax import lax
from jax.experimental import pallas as pl
from jax.experimental.pallas import tpu as pltpu
from jax.sharding import PartitionSpec as P


HD = 64
BLK = 64
NB = 64


def _attend_kernel(p0, nbr_ref, cnt_ref, gain_ref, q_ref, bias_ref, kv_ref, o_ref):
    g = pl.program_id(0)
    width = kv_ref.shape[-1]
    half_w = width // 2
    pairs = half_w // 128
    span = NB * BLK
    live_cols = cnt_ref[g] * BLK
    col = lax.broadcasted_iota(jnp.int32, (BLK, span), 1)
    bias = jnp.where(col < live_cols, bias_ref[0].astype(jnp.float32), -jnp.inf)
    q = q_ref[0]
    lane = lax.broadcasted_iota(jnp.int32, (BLK, 128), 1)
    scale = HD ** (-0.5)
    slots = [nbr_ref[g, j] for j in range(NB)]
    outs = []
    for pair in range(pairs):
        k_lo = pair * 128
        v_lo = half_w + pair * 128
        kp = jnp.concatenate([kv_ref[b, :, k_lo:k_lo + 128] for b in slots], axis=0)
        vp = jnp.concatenate([kv_ref[b, :, v_lo:v_lo + 128] for b in slots], axis=0)
        qp = (q[:, pair * 128:(pair + 1) * 128].astype(jnp.float32) * scale).astype(jnp.bfloat16)
        zeros = jnp.zeros_like(qp)
        q2 = jnp.concatenate(
            [jnp.where(lane < HD, qp, zeros), jnp.where(lane >= HD, qp, zeros)], axis=0
        )
        s2 = lax.dot_general(
            q2, kp, (((1,), (1,)), ((), ())), preferred_element_type=jnp.float32
        )
        ws = []
        sums = []
        for half in range(2):
            h = (p0 + pair) * 2 + half
            s = s2[half * BLK:(half + 1) * BLK] + gain_ref[h] * bias
            top = jnp.max(s, axis=1, keepdims=True)
            expo = jnp.exp(s - top)
            sums.append(jnp.sum(expo, axis=1, keepdims=True))
            ws.append(expo.astype(jnp.bfloat16))
        o2 = jnp.dot(jnp.concatenate(ws, axis=0), vp, preferred_element_type=jnp.float32)
        o2 = o2 * (1.0 / jnp.concatenate(sums, axis=0))
        res = jnp.where(lane < HD, o2[:BLK], o2[BLK:])
        outs.append(res.astype(jnp.bfloat16))
    o_ref[0] = outs[0] if len(outs) == 1 else jnp.concatenate(outs, axis=1)


def attend(nbr, cnt, gain, q_blocks, bias, kv_table, p0, width_q):
    steps = q_blocks.shape[0]
    span = NB * BLK
    grid_spec = pltpu.PrefetchScalarGridSpec(
        num_scalar_prefetch=2,
        grid=(steps,),
        in_specs=[
            pl.BlockSpec(memory_space=pltpu.SMEM),
            pl.BlockSpec((1, BLK, width_q), lambda g, n, c: (g, 0, p0)),
            pl.BlockSpec((1, BLK, span), lambda g, n, c: (g, 0, 0)),
            pl.BlockSpec(kv_table.shape, lambda g, n, c: (0, 0, 0)),
        ],
        out_specs=pl.BlockSpec((1, BLK, width_q), lambda g, n, c: (g, 0, 0)),
    )
    return pl.pallas_call(
        functools.partial(_attend_kernel, p0),
        grid_spec=grid_spec,
        out_shape=jax.ShapeDtypeStruct((steps, BLK, width_q), jnp.bfloat16),
        compiler_params=pltpu.CompilerParams(
            dimension_semantics=("arbitrary",), vmem_limit_bytes=48 * 1024 * 1024
        ),
    )(nbr, cnt, gain, q_blocks, bias, kv_table)


def plan_requests(neighbours, per_owner, owners):
    owner = neighbours // per_owner
    local = neighbours % per_owner
    flat = neighbours.reshape(-1)
    ids = jnp.arange(owners * per_owner, dtype=jnp.int32)
    present = jnp.any(flat[:, None] == ids[None, :], axis=0).reshape(owners, per_owner)
    lidx = jnp.arange(per_owner, dtype=jnp.int32)[None, :]
    first = jnp.min(jnp.where(present, lidx, per_owner), axis=1)
    first = jnp.where(first == per_owner, 0, first)
    second = jnp.max(jnp.where(present, lidx, -1), axis=1)
    second = jnp.where(second < 0, first, second)
    req = jnp.stack([first, second], axis=1).astype(jnp.int32)
    hit = owner.reshape(-1)[:, None] == jnp.arange(owners, dtype=jnp.int32)[None, :]
    first_of = jnp.sum(jnp.where(hit, first[None, :], 0), axis=1).reshape(owner.shape)
    pos = owner * 2 + (local != first_of).astype(jnp.int32)
    return req, pos.astype(jnp.int32)


def _body(features, w_qkv, w_out, bias_gain, edge_bias, neighbours, counts):
    rows = features.shape[0]
    width_heads = w_qkv.shape[2]
    blocks_dev = rows // BLK
    head_devs = lax.axis_size("head")
    row_devs = lax.axis_size("row")
    me = lax.axis_index("head")
    chunk = 128
    chunks = width_heads // chunk
    req, pos = plan_requests(neighbours, blocks_dev, row_devs)
    wanted = lax.all_to_all(req, "row", 0, 0, tiled=True).reshape(-1)
    queries = jnp.dot(features, w_qkv[0], preferred_element_type=jnp.float32).astype(jnp.bfloat16)
    keys = jnp.dot(features, w_qkv[1], preferred_element_type=jnp.float32).astype(jnp.bfloat16)
    values = jnp.dot(features, w_qkv[2], preferred_element_type=jnp.float32).astype(jnp.bfloat16)
    w_parts = []
    for s in range(1, head_devs):
        target = (me + s) % head_devs
        piece = lax.dynamic_slice_in_dim(w_out, target * width_heads, width_heads, axis=1)
        perm = [(i, (i + s) % head_devs) for i in range(head_devs)]
        w_parts.append(lax.ppermute(piece, "head", perm))
    w_own = lax.dynamic_slice_in_dim(w_out, me * width_heads, width_heads, axis=1)
    q_blocks = queries.reshape(blocks_dev, BLK, width_heads)
    outgoing = []
    for c in range(chunks):
        cols = slice(c * chunk, (c + 1) * chunk)
        kv = jnp.concatenate([keys[:, cols], values[:, cols]], axis=1)
        kv = kv.reshape(blocks_dev, BLK, 2 * chunk)
        outgoing.append(jnp.take(kv, wanted, axis=0, mode="clip"))
    total = None
    table = None
    for c in range(chunks):
        cols = slice(c * chunk, (c + 1) * chunk)
        send = outgoing[c]
        if table is not None:
            table, send = lax.optimization_barrier((table, send))
        table = lax.all_to_all(send, "row", 0, 0, tiled=True)
        att = attend(pos, counts, bias_gain, q_blocks, edge_bias, table, c, chunk)
        att = att.reshape(rows, chunk)
        if c + 1 < chunks:
            att_all = [att]
            w_all = [w_own[cols]]
            for s in range(1, head_devs):
                perm = [(i, (i + s) % head_devs) for i in range(head_devs)]
                att_all.append(lax.ppermute(att, "head", perm))
                w_all.append(w_parts[s - 1][cols])
            part = jnp.dot(
                jnp.concatenate(att_all, axis=1),
                jnp.concatenate(w_all, axis=0),
                preferred_element_type=jnp.float32,
            )
        else:
            by_shift = jnp.stack([w_own[cols]] + [w[cols] for w in w_parts])
            order = (me - jnp.arange(head_devs, dtype=jnp.int32)) % head_devs
            by_device = jnp.take(by_shift, order, axis=0, mode="clip")
            rep = jnp.broadcast_to(att[None], (head_devs,) + att.shape)
            recv = lax.all_to_all(rep, "head", 0, 0, tiled=True)
            part = lax.dot_general(
                recv, by_device, (((0, 2), (0, 1)), ((), ())),
                preferred_element_type=jnp.float32,
            )
        total = part if total is None else total + part
    return total.astype(jnp.bfloat16)


def solution(mesh):
    in_specs = (
        P("row", None),
        P(None, None, "head"),
        P("head", None),
        P("head"),
        P("row", None, None),
        P("row", None),
        P("row"),
    )
    out_specs = P("row", "head")
    return jax.shard_map(_body, mesh=mesh, in_specs=in_specs, out_specs=out_specs, check_vma=False)
```

```python
import functools

import jax
import jax.numpy as jnp
from jax import lax
from jax.experimental import pallas as pl
from jax.experimental.pallas import tpu as pltpu
from jax.sharding import PartitionSpec as P


HD = 64
BLK = 64
NB = 64


def _attend_kernel(p0, nbr_ref, cnt_ref, gain_ref, q_ref, bias_ref, kv_ref, o_ref):
    g = pl.program_id(0)
    width = kv_ref.shape[-1]
    half_w = width // 2
    pairs = half_w // 128
    span = NB * BLK
    live_cols = cnt_ref[g] * BLK
    col = lax.broadcasted_iota(jnp.int32, (BLK, span), 1)
    bias = jnp.where(col < live_cols, bias_ref[0].astype(jnp.float32), -jnp.inf)
    q = q_ref[0]
    lane = lax.broadcasted_iota(jnp.int32, (BLK, 128), 1)
    scale = HD ** (-0.5)
    slots = [nbr_ref[g, j] for j in range(NB)]
    outs = []
    for pair in range(pairs):
        k_lo = pair * 128
        v_lo = half_w + pair * 128
        kp = jnp.concatenate([kv_ref[b, :, k_lo:k_lo + 128] for b in slots], axis=0)
        vp = jnp.concatenate([kv_ref[b, :, v_lo:v_lo + 128] for b in slots], axis=0)
        qp = (q[:, pair * 128:(pair + 1) * 128].astype(jnp.float32) * scale).astype(jnp.bfloat16)
        zeros = jnp.zeros_like(qp)
        q2 = jnp.concatenate(
            [jnp.where(lane < HD, qp, zeros), jnp.where(lane >= HD, qp, zeros)], axis=0
        )
        s2 = lax.dot_general(
            q2, kp, (((1,), (1,)), ((), ())), preferred_element_type=jnp.float32
        )
        ws = []
        sums = []
        for half in range(2):
            h = (p0 + pair) * 2 + half
            s = s2[half * BLK:(half + 1) * BLK] + gain_ref[h] * bias
            top = jnp.max(s, axis=1, keepdims=True)
            expo = jnp.exp(s - top)
            sums.append(jnp.sum(expo, axis=1, keepdims=True))
            ws.append(expo.astype(jnp.bfloat16))
        o2 = jnp.dot(jnp.concatenate(ws, axis=0), vp, preferred_element_type=jnp.float32)
        o2 = o2 * (1.0 / jnp.concatenate(sums, axis=0))
        res = jnp.where(lane < HD, o2[:BLK], o2[BLK:])
        outs.append(res.astype(jnp.bfloat16))
    o_ref[0] = outs[0] if len(outs) == 1 else jnp.concatenate(outs, axis=1)


def attend(nbr, cnt, gain, q_blocks, bias, kv_table, p0, width_q):
    steps = q_blocks.shape[0]
    span = NB * BLK
    grid_spec = pltpu.PrefetchScalarGridSpec(
        num_scalar_prefetch=2,
        grid=(steps,),
        in_specs=[
            pl.BlockSpec(memory_space=pltpu.SMEM),
            pl.BlockSpec((1, BLK, width_q), lambda g, n, c: (g, 0, p0)),
            pl.BlockSpec((1, BLK, span), lambda g, n, c: (g, 0, 0)),
            pl.BlockSpec(kv_table.shape, lambda g, n, c: (0, 0, 0)),
        ],
        out_specs=pl.BlockSpec((1, BLK, width_q), lambda g, n, c: (g, 0, 0)),
    )
    return pl.pallas_call(
        functools.partial(_attend_kernel, p0),
        grid_spec=grid_spec,
        out_shape=jax.ShapeDtypeStruct((steps, BLK, width_q), jnp.bfloat16),
        compiler_params=pltpu.CompilerParams(
            dimension_semantics=("arbitrary",), vmem_limit_bytes=48 * 1024 * 1024
        ),
    )(nbr, cnt, gain, q_blocks, bias, kv_table)


def plan_requests(neighbours, per_owner, owners):
    owner = neighbours // per_owner
    local = neighbours % per_owner
    flat = neighbours.reshape(-1)
    ids = jnp.arange(owners * per_owner, dtype=jnp.int32)
    present = jnp.any(flat[:, None] == ids[None, :], axis=0).reshape(owners, per_owner)
    lidx = jnp.arange(per_owner, dtype=jnp.int32)[None, :]
    first = jnp.min(jnp.where(present, lidx, per_owner), axis=1)
    first = jnp.where(first == per_owner, 0, first)
    second = jnp.max(jnp.where(present, lidx, -1), axis=1)
    second = jnp.where(second < 0, first, second)
    req = jnp.stack([first, second], axis=1).astype(jnp.int32)
    hit = owner.reshape(-1)[:, None] == jnp.arange(owners, dtype=jnp.int32)[None, :]
    first_of = jnp.sum(jnp.where(hit, first[None, :], 0), axis=1).reshape(owner.shape)
    pos = owner * 2 + (local != first_of).astype(jnp.int32)
    return req, pos.astype(jnp.int32)


def _body(features, w_qkv, w_out, bias_gain, edge_bias, neighbours, counts):
    rows = features.shape[0]
    width_heads = w_qkv.shape[2]
    blocks_dev = rows // BLK
    head_devs = lax.axis_size("head")
    row_devs = lax.axis_size("row")
    me = lax.axis_index("head")
    chunk = 128
    chunks = width_heads // chunk
    req, pos = plan_requests(neighbours, blocks_dev, row_devs)
    wanted = lax.all_to_all(req, "row", 0, 0, tiled=True).reshape(-1)
    queries = jnp.dot(features, w_qkv[0], preferred_element_type=jnp.float32).astype(jnp.bfloat16)
    keys = jnp.dot(features, w_qkv[1], preferred_element_type=jnp.float32).astype(jnp.bfloat16)
    values = jnp.dot(features, w_qkv[2], preferred_element_type=jnp.float32).astype(jnp.bfloat16)
    w_parts = []
    for s in range(1, head_devs):
        target = (me + s) % head_devs
        piece = lax.dynamic_slice_in_dim(w_out, target * width_heads, width_heads, axis=1)
        perm = [(i, (i + s) % head_devs) for i in range(head_devs)]
        w_parts.append(lax.ppermute(piece, "head", perm))
    w_own = lax.dynamic_slice_in_dim(w_out, me * width_heads, width_heads, axis=1)
    q_blocks = queries.reshape(blocks_dev, BLK, width_heads)
    outgoing = []
    for c in range(chunks):
        cols = slice(c * chunk, (c + 1) * chunk)
        kv = jnp.concatenate([keys[:, cols], values[:, cols]], axis=1)
        kv = kv.reshape(blocks_dev, BLK, 2 * chunk)
        pick = (wanted[:, None] == jnp.arange(blocks_dev, dtype=jnp.int32)[None, :])
        picked = jnp.dot(
            pick.astype(jnp.bfloat16), kv.reshape(blocks_dev, -1),
            preferred_element_type=jnp.float32,
        )
        outgoing.append(picked.astype(jnp.bfloat16).reshape((-1,) + kv.shape[1:]))
    total = None
    table = None
    for c in range(chunks):
        cols = slice(c * chunk, (c + 1) * chunk)
        send = outgoing[c]
        if table is not None:
            table, send = lax.optimization_barrier((table, send))
        table = lax.all_to_all(send, "row", 0, 0, tiled=True)
        att = attend(pos, counts, bias_gain, q_blocks, edge_bias, table, c, chunk)
        att = att.reshape(rows, chunk)
        if c + 1 < chunks:
            att_all = [att]
            w_all = [w_own[cols]]
            for s in range(1, head_devs):
                perm = [(i, (i + s) % head_devs) for i in range(head_devs)]
                att_all.append(lax.ppermute(att, "head", perm))
                w_all.append(w_parts[s - 1][cols])
            part = jnp.dot(
                jnp.concatenate(att_all, axis=1),
                jnp.concatenate(w_all, axis=0),
                preferred_element_type=jnp.float32,
            )
        else:
            by_shift = jnp.stack([w_own[cols]] + [w[cols] for w in w_parts])
            order = (me - jnp.arange(head_devs, dtype=jnp.int32)) % head_devs
            by_device = jnp.take(by_shift, order, axis=0, mode="clip")
            rep = jnp.broadcast_to(att[None], (head_devs,) + att.shape)
            recv = lax.all_to_all(rep, "head", 0, 0, tiled=True)
            part = lax.dot_general(
                recv, by_device, (((0, 2), (0, 1)), ((), ())),
                preferred_element_type=jnp.float32,
            )
        total = part if total is None else total + part
    return total.astype(jnp.bfloat16)


def solution(mesh):
    in_specs = (
        P("row", None),
        P(None, None, "head"),
        P("head", None),
        P("head"),
        P("row", None, None),
        P("row", None),
        P("row"),
    )
    out_specs = P("row", "head")
    return jax.shard_map(_body, mesh=mesh, in_specs=in_specs, out_specs=out_specs, check_vma=False)
```

```python
import functools

import jax
import jax.numpy as jnp
from jax import lax
from jax.experimental import pallas as pl
from jax.experimental.pallas import tpu as pltpu
from jax.sharding import PartitionSpec as P


HD = 64
BLK = 64
NB = 64


def _attend_kernel(p0, masked, nbr_ref, cnt_ref, gain_ref, q_ref, bias_ref, kv_ref, o_ref, *extra):
    g = pl.program_id(0)
    width = kv_ref.shape[-1]
    half_w = width // 2
    pairs = half_w // 128
    span = NB * BLK
    live_cols = cnt_ref[g] * BLK
    col = lax.broadcasted_iota(jnp.int32, (BLK, span), 1)
    if masked:
        bias = bias_ref[0].astype(jnp.float32)
    else:
        bias_m = jnp.where(col < live_cols, bias_ref[0], jnp.asarray(-jnp.inf, bias_ref.dtype))
        extra[0][0] = bias_m
        bias = bias_m.astype(jnp.float32)
    q = q_ref[0]
    lane = lax.broadcasted_iota(jnp.int32, (BLK, 128), 1)
    scale = HD ** (-0.5)
    slots = [nbr_ref[g, j] for j in range(NB)]
    outs = []
    for pair in range(pairs):
        k_lo = pair * 128
        v_lo = half_w + pair * 128
        kp = jnp.concatenate([kv_ref[b, :, k_lo:k_lo + 128] for b in slots], axis=0)
        vp = jnp.concatenate([kv_ref[b, :, v_lo:v_lo + 128] for b in slots], axis=0)
        qp = (q[:, pair * 128:(pair + 1) * 128].astype(jnp.float32) * scale).astype(jnp.bfloat16)
        zeros = jnp.zeros_like(qp)
        q2 = jnp.concatenate(
            [jnp.where(lane < HD, qp, zeros), jnp.where(lane >= HD, qp, zeros)], axis=0
        )
        s2 = lax.dot_general(
            q2, kp, (((1,), (1,)), ((), ())), preferred_element_type=jnp.float32
        )
        ws = []
        sums = []
        for half in range(2):
            h = (p0 + pair) * 2 + half
            s = s2[half * BLK:(half + 1) * BLK] + gain_ref[h] * bias
            top = jnp.max(s, axis=1, keepdims=True)
            expo = jnp.exp(s - top)
            sums.append(jnp.sum(expo, axis=1, keepdims=True))
            ws.append(expo.astype(jnp.bfloat16))
        o2 = jnp.dot(jnp.concatenate(ws, axis=0), vp, preferred_element_type=jnp.float32)
        o2 = o2 * (1.0 / jnp.concatenate(sums, axis=0))
        res = jnp.where(lane < HD, o2[:BLK], o2[BLK:])
        outs.append(res.astype(jnp.bfloat16))
    o_ref[0] = outs[0] if len(outs) == 1 else jnp.concatenate(outs, axis=1)


def attend(nbr, cnt, gain, q_blocks, bias, kv_table, p0, width_q, masked):
    steps = q_blocks.shape[0]
    span = NB * BLK
    grid_spec = pltpu.PrefetchScalarGridSpec(
        num_scalar_prefetch=2,
        grid=(steps,),
        in_specs=[
            pl.BlockSpec(memory_space=pltpu.SMEM),
            pl.BlockSpec((1, BLK, width_q), lambda g, n, c: (g, 0, p0)),
            pl.BlockSpec((1, BLK, span), lambda g, n, c: (g, 0, 0)),
            pl.BlockSpec(kv_table.shape, lambda g, n, c: (0, 0, 0)),
        ],
        out_specs=[pl.BlockSpec((1, BLK, width_q), lambda g, n, c: (g, 0, 0))]
        + ([] if masked else [pl.BlockSpec((1, BLK, span), lambda g, n, c: (g, 0, 0))]),
    )
    return pl.pallas_call(
        functools.partial(_attend_kernel, p0, masked),
        grid_spec=grid_spec,
        out_shape=[jax.ShapeDtypeStruct((steps, BLK, width_q), jnp.bfloat16)]
        + ([] if masked else [jax.ShapeDtypeStruct(bias.shape, bias.dtype)]),
        compiler_params=pltpu.CompilerParams(
            dimension_semantics=("arbitrary",), vmem_limit_bytes=48 * 1024 * 1024
        ),
    )(nbr, cnt, gain, q_blocks, bias, kv_table)


def plan_requests(neighbours, per_owner, owners):
    owner = neighbours // per_owner
    local = neighbours % per_owner
    flat = neighbours.reshape(-1)
    ids = jnp.arange(owners * per_owner, dtype=jnp.int32)
    present = jnp.any(flat[:, None] == ids[None, :], axis=0).reshape(owners, per_owner)
    lidx = jnp.arange(per_owner, dtype=jnp.int32)[None, :]
    first = jnp.min(jnp.where(present, lidx, per_owner), axis=1)
    first = jnp.where(first == per_owner, 0, first)
    second = jnp.max(jnp.where(present, lidx, -1), axis=1)
    second = jnp.where(second < 0, first, second)
    req = jnp.stack([first, second], axis=1).astype(jnp.int32)
    hit = owner.reshape(-1)[:, None] == jnp.arange(owners, dtype=jnp.int32)[None, :]
    first_of = jnp.sum(jnp.where(hit, first[None, :], 0), axis=1).reshape(owner.shape)
    pos = owner * 2 + (local != first_of).astype(jnp.int32)
    return req, pos.astype(jnp.int32)


def _body(features, w_qkv, w_out, bias_gain, edge_bias, neighbours, counts):
    rows = features.shape[0]
    width_heads = w_qkv.shape[2]
    blocks_dev = rows // BLK
    head_devs = lax.axis_size("head")
    row_devs = lax.axis_size("row")
    me = lax.axis_index("head")
    chunk = 128
    chunks = width_heads // chunk
    req, pos = plan_requests(neighbours, blocks_dev, row_devs)
    wanted = lax.all_to_all(req, "row", 0, 0, tiled=True).reshape(-1)
    queries = jnp.dot(features, w_qkv[0], preferred_element_type=jnp.float32).astype(jnp.bfloat16)
    keys = jnp.dot(features, w_qkv[1], preferred_element_type=jnp.float32).astype(jnp.bfloat16)
    values = jnp.dot(features, w_qkv[2], preferred_element_type=jnp.float32).astype(jnp.bfloat16)
    w_parts = []
    for s in range(1, head_devs):
        target = (me + s) % head_devs
        piece = lax.dynamic_slice_in_dim(w_out, target * width_heads, width_heads, axis=1)
        perm = [(i, (i + s) % head_devs) for i in range(head_devs)]
        w_parts.append(lax.ppermute(piece, "head", perm))
    w_own = lax.dynamic_slice_in_dim(w_out, me * width_heads, width_heads, axis=1)
    q_blocks = queries.reshape(blocks_dev, BLK, width_heads)
    outgoing = []
    for c in range(chunks):
        cols = slice(c * chunk, (c + 1) * chunk)
        kv = jnp.concatenate([keys[:, cols], values[:, cols]], axis=1)
        kv = kv.reshape(blocks_dev, BLK, 2 * chunk)
        outgoing.append(jnp.take(kv, wanted, axis=0, mode="clip"))
    total = None
    table = None
    bias_in = edge_bias
    for c in range(chunks):
        cols = slice(c * chunk, (c + 1) * chunk)
        send = outgoing[c]
        if table is not None:
            table, send = lax.optimization_barrier((table, send))
        table = lax.all_to_all(send, "row", 0, 0, tiled=True)
        outs = attend(pos, counts, bias_gain, q_blocks, bias_in, table, c, chunk, c > 0)
        att = outs[0]
        if c == 0:
            bias_in = outs[1]
        att = att.reshape(rows, chunk)
        if c + 1 < chunks:
            att_all = [att]
            w_all = [w_own[cols]]
            for s in range(1, head_devs):
                perm = [(i, (i + s) % head_devs) for i in range(head_devs)]
                att_all.append(lax.ppermute(att, "head", perm))
                w_all.append(w_parts[s - 1][cols])
            part = jnp.dot(
                jnp.concatenate(att_all, axis=1),
                jnp.concatenate(w_all, axis=0),
                preferred_element_type=jnp.float32,
            )
        else:
            by_shift = jnp.stack([w_own[cols]] + [w[cols] for w in w_parts])
            order = (me - jnp.arange(head_devs, dtype=jnp.int32)) % head_devs
            by_device = jnp.take(by_shift, order, axis=0, mode="clip")
            rep = jnp.broadcast_to(att[None], (head_devs,) + att.shape)
            recv = lax.all_to_all(rep, "head", 0, 0, tiled=True)
            part = lax.dot_general(
                recv, by_device, (((0, 2), (0, 1)), ((), ())),
                preferred_element_type=jnp.float32,
            )
        total = part if total is None else total + part
    return total.astype(jnp.bfloat16)


def solution(mesh):
    in_specs = (
        P("row", None),
        P(None, None, "head"),
        P("head", None),
        P("head"),
        P("row", None, None),
        P("row", None),
        P("row"),
    )
    out_specs = P("row", "head")
    return jax.shard_map(_body, mesh=mesh, in_specs=in_specs, out_specs=out_specs, check_vma=False)
```

```python
import functools

import jax
import jax.numpy as jnp
from jax import lax
from jax.experimental import pallas as pl
from jax.experimental.pallas import tpu as pltpu
from jax.sharding import PartitionSpec as P


HD = 64
BLK = 64
NB = 64


def _attend_kernel(p0, nbr_ref, cnt_ref, gain_ref, q_ref, bias_ref, kv_ref, o_ref):
    g = pl.program_id(0)
    width = kv_ref.shape[-1]
    half_w = width // 2
    pairs = half_w // 128
    span = NB * BLK
    live_cols = cnt_ref[g] * BLK
    col = lax.broadcasted_iota(jnp.int32, (BLK, span), 1)
    bias = jnp.where(col < live_cols, bias_ref[0].astype(jnp.float32), -jnp.inf)
    q = q_ref[0]
    lane = lax.broadcasted_iota(jnp.int32, (BLK, 128), 1)
    scale = HD ** (-0.5)
    slots = [nbr_ref[g, j] for j in range(NB)]
    outs = []
    for pair in range(pairs):
        k_lo = pair * 128
        v_lo = half_w + pair * 128
        kp = jnp.concatenate([kv_ref[b, :, k_lo:k_lo + 128] for b in slots], axis=0)
        vp = jnp.concatenate([kv_ref[b, :, v_lo:v_lo + 128] for b in slots], axis=0)
        qp = (q[:, pair * 128:(pair + 1) * 128].astype(jnp.float32) * scale).astype(jnp.bfloat16)
        zeros = jnp.zeros_like(qp)
        q2 = jnp.concatenate(
            [jnp.where(lane < HD, qp, zeros), jnp.where(lane >= HD, qp, zeros)], axis=0
        )
        s2 = lax.dot_general(
            q2, kp, (((1,), (1,)), ((), ())), preferred_element_type=jnp.float32
        )
        ws = []
        sums = []
        for half in range(2):
            h = (p0 + pair) * 2 + half
            s = s2[half * BLK:(half + 1) * BLK] + gain_ref[h] * bias
            top = jnp.max(s, axis=1, keepdims=True)
            expo = jnp.exp(s - top)
            sums.append(jnp.sum(expo, axis=1, keepdims=True))
            ws.append(expo.astype(jnp.bfloat16))
        o2 = jnp.dot(jnp.concatenate(ws, axis=0), vp, preferred_element_type=jnp.float32)
        o2 = o2 * (1.0 / jnp.concatenate(sums, axis=0))
        res = jnp.where(lane < HD, o2[:BLK], o2[BLK:])
        outs.append(res.astype(jnp.bfloat16))
    result = outs[0] if len(outs) == 1 else jnp.concatenate(outs, axis=1)
    for r in range(o_ref.shape[0]):
        o_ref[r, 0] = result


def attend(nbr, cnt, gain, q_blocks, bias, kv_table, p0, width_q, reps=1):
    steps = q_blocks.shape[0]
    span = NB * BLK
    grid_spec = pltpu.PrefetchScalarGridSpec(
        num_scalar_prefetch=2,
        grid=(steps,),
        in_specs=[
            pl.BlockSpec(memory_space=pltpu.SMEM),
            pl.BlockSpec((1, BLK, width_q), lambda g, n, c: (g, 0, p0)),
            pl.BlockSpec((1, BLK, span), lambda g, n, c: (g, 0, 0)),
            pl.BlockSpec(kv_table.shape, lambda g, n, c: (0, 0, 0)),
        ],
        out_specs=pl.BlockSpec((reps, 1, BLK, width_q), lambda g, n, c: (0, g, 0, 0)),
    )
    return pl.pallas_call(
        functools.partial(_attend_kernel, p0),
        grid_spec=grid_spec,
        out_shape=jax.ShapeDtypeStruct((reps, steps, BLK, width_q), jnp.bfloat16),
        compiler_params=pltpu.CompilerParams(
            dimension_semantics=("arbitrary",), vmem_limit_bytes=48 * 1024 * 1024
        ),
    )(nbr, cnt, gain, q_blocks, bias, kv_table)


def plan_requests(neighbours, per_owner, owners):
    owner = neighbours // per_owner
    local = neighbours % per_owner
    flat = neighbours.reshape(-1)
    ids = jnp.arange(owners * per_owner, dtype=jnp.int32)
    present = jnp.any(flat[:, None] == ids[None, :], axis=0).reshape(owners, per_owner)
    lidx = jnp.arange(per_owner, dtype=jnp.int32)[None, :]
    first = jnp.min(jnp.where(present, lidx, per_owner), axis=1)
    first = jnp.where(first == per_owner, 0, first)
    second = jnp.max(jnp.where(present, lidx, -1), axis=1)
    second = jnp.where(second < 0, first, second)
    req = jnp.stack([first, second], axis=1).astype(jnp.int32)
    hit = owner.reshape(-1)[:, None] == jnp.arange(owners, dtype=jnp.int32)[None, :]
    first_of = jnp.sum(jnp.where(hit, first[None, :], 0), axis=1).reshape(owner.shape)
    pos = owner * 2 + (local != first_of).astype(jnp.int32)
    return req, pos.astype(jnp.int32)


def _body(features, w_qkv, w_out, bias_gain, edge_bias, neighbours, counts):
    rows = features.shape[0]
    width_heads = w_qkv.shape[2]
    blocks_dev = rows // BLK
    head_devs = lax.axis_size("head")
    row_devs = lax.axis_size("row")
    me = lax.axis_index("head")
    chunk = 128
    chunks = width_heads // chunk
    req, pos = plan_requests(neighbours, blocks_dev, row_devs)
    wanted = lax.all_to_all(req, "row", 0, 0, tiled=True).reshape(-1)
    queries = jnp.dot(features, w_qkv[0], preferred_element_type=jnp.float32).astype(jnp.bfloat16)
    keys = jnp.dot(features, w_qkv[1], preferred_element_type=jnp.float32).astype(jnp.bfloat16)
    values = jnp.dot(features, w_qkv[2], preferred_element_type=jnp.float32).astype(jnp.bfloat16)
    w_parts = []
    for s in range(1, head_devs):
        target = (me + s) % head_devs
        piece = lax.dynamic_slice_in_dim(w_out, target * width_heads, width_heads, axis=1)
        perm = [(i, (i + s) % head_devs) for i in range(head_devs)]
        w_parts.append(lax.ppermute(piece, "head", perm))
    w_own = lax.dynamic_slice_in_dim(w_out, me * width_heads, width_heads, axis=1)
    q_blocks = queries.reshape(blocks_dev, BLK, width_heads)
    outgoing = []
    for c in range(chunks):
        cols = slice(c * chunk, (c + 1) * chunk)
        kv = jnp.concatenate([keys[:, cols], values[:, cols]], axis=1)
        kv = kv.reshape(blocks_dev, BLK, 2 * chunk)
        outgoing.append(jnp.take(kv, wanted, axis=0, mode="clip"))
    total = None
    table = None
    for c in range(chunks):
        cols = slice(c * chunk, (c + 1) * chunk)
        send = outgoing[c]
        if table is not None:
            table, send = lax.optimization_barrier((table, send))
        table = lax.all_to_all(send, "row", 0, 0, tiled=True)
        reps = 1 if c + 1 < chunks else head_devs
        att_rep = attend(pos, counts, bias_gain, q_blocks, edge_bias, table, c, chunk, reps)
        att_rep = att_rep.reshape(reps, rows, chunk)
        att = att_rep[0]
        if c + 1 < chunks:
            att_all = [att]
            w_all = [w_own[cols]]
            for s in range(1, head_devs):
                perm = [(i, (i + s) % head_devs) for i in range(head_devs)]
                att_all.append(lax.ppermute(att, "head", perm))
                w_all.append(w_parts[s - 1][cols])
            part = jnp.dot(
                jnp.concatenate(att_all, axis=1),
                jnp.concatenate(w_all, axis=0),
                preferred_element_type=jnp.float32,
            )
        else:
            by_shift = jnp.stack([w_own[cols]] + [w[cols] for w in w_parts])
            order = (me - jnp.arange(head_devs, dtype=jnp.int32)) % head_devs
            by_device = jnp.take(by_shift, order, axis=0, mode="clip")
            recv = lax.all_to_all(att_rep, "head", 0, 0, tiled=True)
            part = lax.dot_general(
                recv, by_device, (((0, 2), (0, 1)), ((), ())),
                preferred_element_type=jnp.float32,
            )
        total = part if total is None else total + part
    return total.astype(jnp.bfloat16)


def solution(mesh):
    in_specs = (
        P("row", None),
        P(None, None, "head"),
        P("head", None),
        P("head"),
        P("row", None, None),
        P("row", None),
        P("row"),
    )
    out_specs = P("row", "head")
    return jax.shard_map(_body, mesh=mesh, in_specs=in_specs, out_specs=out_specs, check_vma=False)
```
